128 devices in a mesh: blk: 8 (over y_lo, x), dp: 16 (over z, y_hi, core).
Axes of the slice: x: 4, y: 4 (y_hi: 2, y_lo: 2; y = y_hi * 2 + y_lo), z: 4, core: 2. Of those that a mesh axis runs over, the one named last changes fastest.
Arguments:
- train_grads: bfloat16 [8192, 8192], P(('blk', 'dp')), may hold values from -6 to 6
- train_scale: bfloat16 [8192], P(('blk', 'dp')), may hold values from 0.5 to 4
- train_class: int32 [8192], P(('blk', 'dp')), may hold values from 0 to 511
- test_grads: bfloat16 [8192, 8192], P(('blk', 'dp')), may hold values from -0.099609375 to 0.099609375
- test_class: int32 [8192], P(('blk', 'dp')), may hold values from 0 to 511
Outputs:
- train_attr: float32 [8192, 512], P(('blk', 'dp'))
- test_attr: float32 [8192], P(('blk', 'dp'))
The draws below stay inside these ranges and needn't reach their ends.
All inputs are finite; a program needn't handle non-finite values.
Results may differ from the reference program's by a relative error of at most 0.0021.
Values may be sent and summed in bfloat16 or wider, within the bound.
No kernel may reach another device: no remote copies, remote signals or barrier semaphores. Data moves between devices by JAX's collectives and lax.ppermute only.
A program may use at most 128 MiB of HBM per device.

```python
import math
import jax
import jax.numpy as jnp
from jax import lax

K = 8192
NCLS = 512
TR_DEV = 64
NTRAIN = 8192
NTEST = 8192


def plant(values, stream_key, least, largest):
    longest = values.shape.index(max(values.shape))
    spots = []
    for shift in (0, 1):
        where = [jax.random.randint(jax.random.fold_in(stream_key, axis), (), 0, length) for axis, length in enumerate(values.shape)]
        where[longest] = (where[longest] + shift) % values.shape[longest]
        spots.append(tuple(where))
    return values.at[spots[0]].set(least).at[spots[1]].set(largest)


def levels(own_key, shape, pieces, low, high):
    gain = 1.0
    for axis_at, blocks in pieces:
        heights = jax.random.uniform(jax.random.fold_in(jax.random.fold_in(own_key, 6), axis_at), (blocks,), jnp.float32, low / len(pieces), high / len(pieces))
        gain = gain * jnp.repeat(jnp.exp(heights), shape[axis_at] // blocks).reshape((-1,) + (1,) * (len(shape) - 1 - axis_at))
    return gain


def bell_draw(rng, extent, spread, reach, split=(), dtype=jnp.bfloat16):
    factor_of = levels(rng, extent, split, -0.22, 0.18) if split else 1.0
    values = jax.random.normal(rng, extent, jnp.float32) * spread * factor_of
    return jnp.minimum(jnp.maximum(values, -reach), reach).astype(dtype)


def setup_inputs(seed: int = 0) -> dict:
    key_of = jax.random.split(jax.random.key(seed), 6)
    return {
        "train_grads": bell_draw(key_of[0], (NTRAIN, K), 1.0, 6.0, ((0, 128),)),
        "train_scale": jnp.clip(jnp.exp(math.log(4.0) - 2.0794415 * jax.random.uniform(key_of[1], (NTRAIN,), jnp.float32) ** levels(key_of[1], (NTRAIN,), ((0, 128),), -0.2, 0.2)), 0.5, 4.0).astype(jnp.bfloat16),
        "train_class": plant(jax.random.randint(key_of[2], (NTRAIN,), 0, NCLS), jax.random.fold_in(key_of[2], 1), 0, NCLS - 1).astype(jnp.int32),
        "test_grads": bell_draw(key_of[3], (NTEST, K), 0.0166, 0.099609375, ((0, 128),)),
        "test_class": plant(jax.random.randint(key_of[4], (NTEST,), 0, NCLS), jax.random.fold_in(key_of[4], 1), 0, NCLS - 1).astype(jnp.int32),
    }


def indicator(labels):
    columns = lax.broadcasted_iota(jnp.int32, (labels.shape[0], NCLS), 1)
    return (labels[:, None] == columns).astype(jnp.bfloat16)


def reference(train_grads, train_scale, train_class, test_grads, test_class):
    test_hot = indicator(test_class)
    test_hot_wide = test_hot.astype(jnp.float32)
    count = NTRAIN // TR_DEV
    grads_blocks = train_grads.reshape(count, TR_DEV, K)
    scale_blocks = train_scale.reshape(count, TR_DEV)
    class_blocks = train_class.reshape(count, TR_DEV)

    def step(support, block):
        grads, scale, labels = block
        raw = jnp.dot(grads, test_grads.T, preferred_element_type=jnp.float32)
        weights = jnp.tanh(scale.astype(jnp.float32)[:, None] * raw).astype(jnp.bfloat16)
        part = jnp.dot(weights, test_hot, preferred_element_type=jnp.float32)
        per_class = jnp.dot(weights.T, indicator(labels), preferred_element_type=jnp.float32)
        support = support + jnp.sum(per_class * test_hot_wide, axis=1)
        return support, part

    support, parts = lax.scan(step, jnp.zeros((NTEST,), jnp.float32), (grads_blocks, scale_blocks, class_blocks))
    return parts.reshape(NTRAIN, NCLS), support
```

```python
import jax
import jax.numpy as jnp
from jax import lax
from jax.sharding import PartitionSpec as P

NCLS = 512
PAD = 128


def indicator(labels):
    columns = lax.broadcasted_iota(jnp.int32, (labels.shape[0], NCLS), 1)
    return (labels[:, None] == columns).astype(jnp.bfloat16)


def with_side(grads, side, first):
    rows = grads.shape[0]
    cols = lax.broadcasted_iota(jnp.int32, (rows, PAD), 1)
    extra = jnp.zeros((rows, PAD), jnp.bfloat16)
    for k, v in enumerate(side):
        extra = jnp.where(cols == first + k, v[:, None].astype(jnp.bfloat16), extra)
    return jnp.concatenate([grads, extra], axis=1)


def split_class(c):
    return (c // 32, c % 32)


def join_class(x, k):
    hi = x[:, k].astype(jnp.int32)
    lo = x[:, k + 1].astype(jnp.int32)
    return hi * 32 + lo


def local(train_grads, train_scale, train_class, test_grads, test_class):
    k = train_grads.shape[1]
    tr = with_side(train_grads, (train_scale,) + split_class(train_class), 0)
    te = with_side(test_grads, split_class(test_class), 4)
    tr_all = lax.all_gather(tr, "blk", axis=0, tiled=True)
    te_all = lax.all_gather(te, "dp", axis=0, tiled=True)
    raw = lax.dot_general(
        tr_all, te_all, (((1,), (1,)), ((), ())), preferred_element_type=jnp.float32
    )
    scale = tr_all[:, k].astype(jnp.float32)
    weights = jnp.tanh(scale[:, None] * raw).astype(jnp.bfloat16)
    train_hot = indicator(join_class(tr_all, k + 1))
    test_hot = indicator(join_class(te_all, k + 4))
    part = jnp.dot(weights, test_hot, preferred_element_type=jnp.float32)
    per_class = lax.dot_general(
        weights, train_hot, (((0,), (0,)), ((), ())), preferred_element_type=jnp.float32
    )
    test_part = jnp.sum(per_class * test_hot.astype(jnp.float32), axis=1)
    train_attr = lax.psum_scatter(part, "blk", scatter_dimension=0, tiled=True)
    test_attr = lax.psum_scatter(test_part, "dp", scatter_dimension=0, tiled=True)
    return (train_attr, test_attr)


def solution(mesh):
    in_specs = (
        P(("blk", "dp"), None),
        P(("blk", "dp")),
        P(("blk", "dp")),
        P(("blk", "dp"), None),
        P(("blk", "dp")),
    )
    out_specs = (P(("blk", "dp"), None), P(("blk", "dp")))
    return jax.shard_map(local, mesh=mesh, in_specs=in_specs, out_specs=out_specs, check_vma=False)
```

```python
import jax
import jax.numpy as jnp
from jax import lax
from jax.sharding import PartitionSpec as P

NCLS = 512
PAD = 128


def indicator(labels):
    columns = lax.broadcasted_iota(jnp.int32, (labels.shape[0], NCLS), 1)
    return (labels[:, None] == columns).astype(jnp.bfloat16)


def with_side(grads, side, first):
    rows = grads.shape[0]
    cols = lax.broadcasted_iota(jnp.int32, (rows, PAD), 1)
    extra = jnp.zeros((rows, PAD), jnp.bfloat16)
    for k, v in enumerate(side):
        extra = jnp.where(cols == first + k, v[:, None].astype(jnp.bfloat16), extra)
    return jnp.concatenate([grads, extra], axis=1)


def split_class(c):
    return (c // 32, c % 32)


def join_class(x, k):
    hi = x[:, k].astype(jnp.int32)
    lo = x[:, k + 1].astype(jnp.int32)
    return hi * 32 + lo


def blk_pieces(tr, nx, ny):
    n = nx * ny
    yl = lax.axis_index("blk") // nx

    def at(y, x):
        return y * nx + x % nx

    partner = lax.ppermute(tr, "blk", [(at(y, x), at(1 - y, x)) for y in range(ny) for x in range(nx)])
    unit = jnp.where(yl == 0, jnp.concatenate([tr, partner]), jnp.concatenate([partner, tr]))
    right = [(at(y, x), at(y, x + 1)) for y in range(ny) for x in range(nx)]
    left = [(at(y, x), at(y, x - 1)) for y in range(ny) for x in range(nx)]
    from_left = lax.ppermute(unit, "blk", right)
    from_right = lax.ppermute(unit, "blk", left)
    rows = tr.shape[0]
    far_a = lax.ppermute(from_left[:rows], "blk", right)
    far_b = lax.ppermute(from_right[rows:], "blk", left)
    far = jnp.concatenate([far_a, far_b])
    return [unit, from_right, far, from_left]


def local(train_grads, train_scale, train_class, test_grads, test_class):
    k = train_grads.shape[1]
    rows = train_grads.shape[0]
    nx, ny = 4, 2
    tr = with_side(train_grads, (train_scale,) + split_class(train_class), 0)
    te = with_side(test_grads, split_class(test_class), 4)
    te_all = lax.all_gather(te, "dp", axis=0, tiled=True)
    test_hot = indicator(join_class(te_all, k + 4))
    pieces = blk_pieces(tr, nx, ny)
    ws, hots = [], []
    for piece in pieces:
        raw = lax.dot_general(
            piece, te_all, (((1,), (1,)), ((), ())), preferred_element_type=jnp.float32
        )
        scale = piece[:, k].astype(jnp.float32)
        ws.append(jnp.tanh(scale[:, None] * raw).astype(jnp.bfloat16))
        hots.append(indicator(join_class(piece, k + 1)))
    weights = jnp.concatenate(ws)
    train_hot = jnp.concatenate(hots)
    part = jnp.dot(weights, test_hot, preferred_element_type=jnp.float32)
    xc = lax.axis_index("blk") % nx
    part = jnp.roll(part.reshape(nx, ny, rows, NCLS), xc, axis=0)
    part = jnp.swapaxes(part, 0, 1).reshape(nx * ny * rows, NCLS)
    per_class = lax.dot_general(
        weights, train_hot, (((0,), (0,)), ((), ())), preferred_element_type=jnp.float32
    )
    test_part = jnp.sum(per_class * test_hot.astype(jnp.float32), axis=1)
    train_attr = lax.psum_scatter(part, "blk", scatter_dimension=0, tiled=True)
    test_attr = lax.psum_scatter(test_part, "dp", scatter_dimension=0, tiled=True)
    return (train_attr, test_attr)


def solution(mesh):
    in_specs = (
        P(("blk", "dp"), None),
        P(("blk", "dp")),
        P(("blk", "dp")),
        P(("blk", "dp"), None),
        P(("blk", "dp")),
    )
    out_specs = (P(("blk", "dp"), None), P(("blk", "dp")))
    return jax.shard_map(local, mesh=mesh, in_specs=in_specs, out_specs=out_specs, check_vma=False)
```

```python
import jax
import jax.numpy as jnp
from jax import lax
from jax.sharding import PartitionSpec as P

NCLS = 512
PAD = 128


def indicator(labels):
    columns = lax.broadcasted_iota(jnp.int32, (labels.shape[0], NCLS), 1)
    return (labels[:, None] == columns).astype(jnp.bfloat16)


def with_side(grads, side, first):
    rows = grads.shape[0]
    cols = lax.broadcasted_iota(jnp.int32, (rows, PAD), 1)
    extra = jnp.zeros((rows, PAD), jnp.bfloat16)
    for k, v in enumerate(side):
        extra = jnp.where(cols == first + k, v[:, None].astype(jnp.bfloat16), extra)
    return jnp.concatenate([grads, extra], axis=1)


def split_class(c):
    return (c // 32, c % 32)


def join_class(x, k):
    hi = x[:, k].astype(jnp.int32)
    lo = x[:, k + 1].astype(jnp.int32)
    return hi * 32 + lo


def blk_pieces(tr, nx, ny):
    n = nx * ny
    yl = lax.axis_index("blk") // nx

    def at(y, x):
        return y * nx + x % nx

    partner = lax.ppermute(tr, "blk", [(at(y, x), at(1 - y, x)) for y in range(ny) for x in range(nx)])
    unit = jnp.where(yl == 0, jnp.concatenate([tr, partner]), jnp.concatenate([partner, tr]))
    right = [(at(y, x), at(y, x + 1)) for y in range(ny) for x in range(nx)]
    left = [(at(y, x), at(y, x - 1)) for y in range(ny) for x in range(nx)]
    from_left = lax.ppermute(unit, "blk", right)
    from_right = lax.ppermute(unit, "blk", left)
    rows = tr.shape[0]
    far_a = lax.ppermute(from_left[:rows], "blk", right)
    far_b = lax.ppermute(from_right[rows:], "blk", left)
    far = jnp.concatenate([far_a, far_b])
    return [unit, from_right, far, from_left]


def local(train_grads, train_scale, train_class, test_grads, test_class):
    k = train_grads.shape[1]
    rows = train_grads.shape[0]
    nx, ny = 4, 2
    tr = with_side(train_grads, (train_scale,) + split_class(train_class), 0)
    te = with_side(test_grads, split_class(test_class), 4)
    te_all = lax.all_gather(te, "dp", axis=0, tiled=True)
    test_hot = indicator(join_class(te_all, k + 4))
    pieces = blk_pieces(tr, nx, ny)
    train_all = jnp.concatenate(pieces)
    raw = lax.dot_general(
        train_all, te_all, (((1,), (1,)), ((), ())), preferred_element_type=jnp.float32
    )
    scale = train_all[:, k].astype(jnp.float32)
    weights = jnp.tanh(scale[:, None] * raw).astype(jnp.bfloat16)
    train_hot = indicator(join_class(train_all, k + 1))
    part = jnp.dot(weights, test_hot, preferred_element_type=jnp.float32)
    xc = lax.axis_index("blk") % nx
    part = jnp.roll(part.reshape(nx, ny, rows, NCLS), xc, axis=0)
    part = jnp.swapaxes(part, 0, 1).reshape(nx * ny * rows, NCLS)
    per_class = lax.dot_general(
        weights, train_hot, (((0,), (0,)), ((), ())), preferred_element_type=jnp.float32
    )
    test_part = jnp.sum(per_class * test_hot.astype(jnp.float32), axis=1)
    train_attr = lax.psum_scatter(part, "blk", scatter_dimension=0, tiled=True)
    test_attr = lax.psum_scatter(test_part, "dp", scatter_dimension=0, tiled=True)
    return (train_attr, test_attr)


def solution(mesh):
    in_specs = (
        P(("blk", "dp"), None),
        P(("blk", "dp")),
        P(("blk", "dp")),
        P(("blk", "dp"), None),
        P(("blk", "dp")),
    )
    out_specs = (P(("blk", "dp"), None), P(("blk", "dp")))
    return jax.shard_map(local, mesh=mesh, in_specs=in_specs, out_specs=out_specs, check_vma=False)
```

```python
import jax
import jax.numpy as jnp
from jax import lax
from jax.sharding import PartitionSpec as P

NCLS = 512
PAD = 128
AXES = ("blk", "dp")


def indicator(labels):
    columns = lax.broadcasted_iota(jnp.int32, (labels.shape[0], NCLS), 1)
    return (labels[:, None] == columns).astype(jnp.bfloat16)


def with_side(grads, side, first):
    rows = grads.shape[0]
    cols = lax.broadcasted_iota(jnp.int32, (rows, PAD), 1)
    extra = jnp.zeros((rows, PAD), jnp.bfloat16)
    for k, v in enumerate(side):
        extra = jnp.where(cols == first + k, v[:, None].astype(jnp.bfloat16), extra)
    return jnp.concatenate([grads, extra], axis=1)


def split_class(c):
    return (c // 32, c % 32)


def join_class(x, k):
    hi = x[:, k].astype(jnp.int32)
    lo = x[:, k + 1].astype(jnp.int32)
    return hi * 32 + lo


def coords(L):
    blk, dp = divmod(L, 16)
    yl, x = divmod(blk, 4)
    z, r = divmod(dp, 4)
    yh, c = divmod(r, 2)
    return [x, 2 * yh + yl, z], c


def lin(v, c):
    x, y, z = v
    return ((y % 2) * 4 + x) * 16 + z * 4 + (y // 2) * 2 + c


def train_mate(v):
    return v ^ 1


def test_mate(v):
    return ((((v - 1) % 4) ^ 1) + 1) % 4


def mate_pairs(n, axis, mate):
    out = []
    for L in range(n):
        v, c = coords(L)
        w = list(v)
        w[axis] = mate(v[axis])
        out.append((L, lin(w, c)))
    return out


def core_pairs(n):
    return [(L, L ^ 1) for L in range(n)]


def cube_gather(shard, mate, n):
    cols = shard.shape[1]
    tiles = cols // 128
    cut = [0, (tiles // 3) * 128, (2 * tiles // 3) * 128, cols]
    parts = []
    for p in range(3):
        order = [(p + s) % 3 for s in range(3)]
        buf = [shard[:, cut[p]:cut[p + 1]]]
        labs = [0]
        for a in order:
            got = lax.ppermute(buf, AXES, mate_pairs(n, a, mate))
            buf = buf + list(got)
            labs = labs + [o ^ (1 << a) for o in labs]
        parts.append({o: b for o, b in zip(labs, buf)})
    return jnp.concatenate(
        [jnp.concatenate([parts[p][o] for p in range(3)], axis=1) for o in range(8)]
    )


def cube_reduce(blocks, mate, n):
    blocks = list(blocks)
    live = list(range(8))
    for a in range(3):
        send = [o for o in live if o & (1 << a)]
        keep = [o for o in live if not o & (1 << a)]
        got = lax.ppermute([blocks[o] for o in send], AXES, mate_pairs(n, a, mate))
        for o, g in zip(send, got):
            blocks[o ^ (1 << a)] = blocks[o ^ (1 << a)] + g
        live = keep
    return blocks[0]


def local(train_grads, train_scale, train_class, test_grads, test_class):
    n = 128
    k = train_grads.shape[1]
    rows = train_grads.shape[0]
    tr = with_side(train_grads, (train_scale,) + split_class(train_class), 0)
    te = with_side(test_grads, split_class(test_class), 4)
    te_all = cube_gather(te, test_mate, n)
    tr_mine = cube_gather(tr, train_mate, n)
    tr_other = lax.ppermute(tr_mine, AXES, core_pairs(n))
    test_hot = indicator(join_class(te_all, k + 4))

    def weigh(t):
        raw = lax.dot_general(
            t, te_all, (((1,), (1,)), ((), ())), preferred_element_type=jnp.float32
        )
        scale = t[:, k].astype(jnp.float32)
        w = jnp.tanh(scale[:, None] * raw).astype(jnp.bfloat16)
        hot = indicator(join_class(t, k + 1))
        part = jnp.dot(w, test_hot, preferred_element_type=jnp.float32)
        per_class = lax.dot_general(
            w, hot, (((0,), (0,)), ((), ())), preferred_element_type=jnp.float32
        )
        return part, per_class

    part_m, pc_m = weigh(tr_mine)
    part_o, pc_o = weigh(tr_other)
    part = part_m + lax.ppermute(part_o, AXES, core_pairs(n))
    train_attr = cube_reduce(
        [part[o * rows:(o + 1) * rows] for o in range(8)], train_mate, n
    )
    test_part = jnp.sum((pc_m + pc_o) * test_hot.astype(jnp.float32), axis=1)
    test_attr = cube_reduce(
        [test_part[o * rows:(o + 1) * rows] for o in range(8)], test_mate, n
    )
    return (train_attr, test_attr)


def solution(mesh):
    in_specs = (
        P(AXES, None),
        P(AXES),
        P(AXES),
        P(AXES, None),
        P(AXES),
    )
    out_specs = (P(AXES, None), P(AXES))
    return jax.shard_map(local, mesh=mesh, in_specs=in_specs, out_specs=out_specs, check_vma=False)
```

```python
import jax
import jax.numpy as jnp
from jax import lax
from jax.sharding import PartitionSpec as P

NCLS = 512
PAD = 128
AXES = ("blk", "dp")


def indicator(labels):
    columns = lax.broadcasted_iota(jnp.int32, (labels.shape[0], NCLS), 1)
    return (labels[:, None] == columns).astype(jnp.bfloat16)


def with_side(grads, side, first):
    rows = grads.shape[0]
    cols = lax.broadcasted_iota(jnp.int32, (rows, PAD), 1)
    extra = jnp.zeros((rows, PAD), jnp.bfloat16)
    for k, v in enumerate(side):
        extra = jnp.where(cols == first + k, v[:, None].astype(jnp.bfloat16), extra)
    return jnp.concatenate([grads, extra], axis=1)


def split_class(c):
    return (c // 32, c % 32)


def join_class(x, k):
    hi = x[:, k].astype(jnp.int32)
    lo = x[:, k + 1].astype(jnp.int32)
    return hi * 32 + lo


def coords(L):
    blk, dp = divmod(L, 16)
    yl, x = divmod(blk, 4)
    z, r = divmod(dp, 4)
    yh, c = divmod(r, 2)
    return [x, 2 * yh + yl, z], c


def lin(v, c):
    x, y, z = v
    return ((y % 2) * 4 + x) * 16 + z * 4 + (y // 2) * 2 + c


def train_mate(v):
    return v ^ 1


def test_mate(v):
    return ((((v - 1) % 4) ^ 1) + 1) % 4


def mate_pairs(n, axis, mate):
    out = []
    for L in range(n):
        v, c = coords(L)
        w = list(v)
        w[axis] = mate(v[axis])
        out.append((L, lin(w, c)))
    return out


def core_pairs(n):
    return [(L, L ^ 1) for L in range(n)]


def cube_gather(shard, mate, n):
    cols = shard.shape[1]
    tiles = cols // 128
    cut = [0, (tiles // 3) * 128, (2 * tiles // 3) * 128, cols]
    parts = []
    for p in range(3):
        order = [(p + s) % 3 for s in range(3)]
        buf = shard[:, cut[p]:cut[p + 1]]
        labs = [0]
        for a in order:
            got = lax.ppermute(buf, AXES, mate_pairs(n, a, mate))
            buf = jnp.concatenate([buf, got])
            labs = labs + [o ^ (1 << a) for o in labs]
        rows = shard.shape[0]
        parts.append({o: buf[i * rows:(i + 1) * rows] for i, o in enumerate(labs)})
    return jnp.concatenate(
        [jnp.concatenate([parts[p][o] for p in range(3)], axis=1) for o in range(8)]
    )


def cube_reduce(blocks, mate, n):
    blocks = list(blocks)
    live = list(range(8))
    for a in range(3):
        send = [o for o in live if o & (1 << a)]
        keep = [o for o in live if not o & (1 << a)]
        rows = blocks[0].shape[0]
        got = lax.ppermute(
            jnp.concatenate([blocks[o] for o in send]), AXES, mate_pairs(n, a, mate)
        )
        for i, o in enumerate(send):
            blocks[o ^ (1 << a)] = blocks[o ^ (1 << a)] + got[i * rows:(i + 1) * rows]
        live = keep
    return blocks[0]


def local(train_grads, train_scale, train_class, test_grads, test_class):
    n = 128
    k = train_grads.shape[1]
    rows = train_grads.shape[0]
    tr = with_side(train_grads, (train_scale,) + split_class(train_class), 0)
    te = with_side(test_grads, split_class(test_class), 4)
    te_all = cube_gather(te, test_mate, n)
    tr_mine = cube_gather(tr, train_mate, n)
    tr_other = lax.ppermute(tr_mine, AXES, core_pairs(n))
    test_hot = indicator(join_class(te_all, k + 4))

    def weigh(t):
        raw = lax.dot_general(
            t, te_all, (((1,), (1,)), ((), ())), preferred_element_type=jnp.float32
        )
        scale = t[:, k].astype(jnp.float32)
        w = jnp.tanh(scale[:, None] * raw).astype(jnp.bfloat16)
        hot = indicator(join_class(t, k + 1))
        part = jnp.dot(w, test_hot, preferred_element_type=jnp.float32)
        per_class = lax.dot_general(
            w, hot, (((0,), (0,)), ((), ())), preferred_element_type=jnp.float32
        )
        return part, per_class

    part_m, pc_m = weigh(tr_mine)
    part_o, pc_o = weigh(tr_other)
    part = part_m + lax.ppermute(part_o, AXES, core_pairs(n))
    train_attr = cube_reduce(
        [part[o * rows:(o + 1) * rows] for o in range(8)], train_mate, n
    )
    test_part = jnp.sum((pc_m + pc_o) * test_hot.astype(jnp.float32), axis=1)
    test_attr = cube_reduce(
        [test_part[o * rows:(o + 1) * rows] for o in range(8)], test_mate, n
    )
    return (train_attr, test_attr)


def solution(mesh):
    in_specs = (
        P(AXES, None),
        P(AXES),
        P(AXES),
        P(AXES, None),
        P(AXES),
    )
    out_specs = (P(AXES, None), P(AXES))
    return jax.shard_map(local, mesh=mesh, in_specs=in_specs, out_specs=out_specs, check_vma=False)
```

```python
import jax
import jax.numpy as jnp
from jax import lax
from jax.sharding import PartitionSpec as P

NCLS = 512
PAD = 128
AXES = ("blk", "dp")


def indicator(labels):
    columns = lax.broadcasted_iota(jnp.int32, (labels.shape[0], NCLS), 1)
    return (labels[:, None] == columns).astype(jnp.bfloat16)


def with_side(grads, side, first):
    rows = grads.shape[0]
    cols = lax.broadcasted_iota(jnp.int32, (rows, PAD), 1)
    extra = jnp.zeros((rows, PAD), jnp.bfloat16)
    for k, v in enumerate(side):
        extra = jnp.where(cols == first + k, v[:, None].astype(jnp.bfloat16), extra)
    return jnp.concatenate([grads, extra], axis=1)


def split_class(c):
    return (c // 32, c % 32)


def join_class(x, k):
    hi = x[:, k].astype(jnp.int32)
    lo = x[:, k + 1].astype(jnp.int32)
    return hi * 32 + lo


def coords(L):
    blk, dp = divmod(L, 16)
    yl, x = divmod(blk, 4)
    z, r = divmod(dp, 4)
    yh, c = divmod(r, 2)
    return [x, 2 * yh + yl, z], c


def lin(v, c):
    x, y, z = v
    return ((y % 2) * 4 + x) * 16 + z * 4 + (y // 2) * 2 + c


def train_mate(v):
    return v ^ 1


def test_mate(v):
    return ((((v - 1) % 4) ^ 1) + 1) % 4


def mate_pairs(n, axis, mate):
    out = []
    for L in range(n):
        v, c = coords(L)
        w = list(v)
        w[axis] = mate(v[axis])
        out.append((L, lin(w, c)))
    return out


def core_pairs(n):
    return [(L, L ^ 1) for L in range(n)]


def cube_parts(shard, mate, n):
    cols = shard.shape[1]
    rows = shard.shape[0]
    tiles = cols // 128
    cut = [0, (tiles // 3) * 128, (2 * tiles // 3) * 128, cols]
    parts = []
    for p in range(3):
        order = [(p + s) % 3 for s in range(3)]
        buf = shard[:, cut[p]:cut[p + 1]]
        labs = [0]
        for a in order:
            got = lax.ppermute(buf, AXES, mate_pairs(n, a, mate))
            buf = jnp.concatenate([buf, got])
            labs = labs + [o ^ (1 << a) for o in labs]
        at = {o: i for i, o in enumerate(labs)}
        parts.append(jnp.concatenate([buf[at[o] * rows:(at[o] + 1) * rows] for o in range(8)]))
    return parts


def offset_pairs(n, o, mate):
    out = []
    for L in range(n):
        v, c = coords(L)
        w = [mate(v[a]) if o & (1 << a) else v[a] for a in range(3)]
        out.append((L, lin(w, c)))
    return out


def cube_reduce(blocks, mate, n):
    total = blocks[0]
    for o in range(1, 8):
        total = total + lax.ppermute(blocks[o], AXES, offset_pairs(n, o, mate))
    return total


def local(train_grads, train_scale, train_class, test_grads, test_class):
    n = 128
    k = train_grads.shape[1]
    rows = train_grads.shape[0]
    tr = with_side(train_grads, (train_scale,) + split_class(train_class), 0)
    te = with_side(test_grads, split_class(test_class), 4)
    te_all = jnp.concatenate(cube_parts(te, test_mate, n), axis=1)
    tr_parts = cube_parts(tr, train_mate, n)
    tr_mine = jnp.concatenate(tr_parts, axis=1)
    tr_other = jnp.concatenate(
        [lax.ppermute(t, AXES, core_pairs(n)) for t in tr_parts], axis=1
    )
    test_hot = indicator(join_class(te_all, k + 4))

    def weigh(t):
        raw = lax.dot_general(
            t, te_all, (((1,), (1,)), ((), ())), preferred_element_type=jnp.float32
        )
        scale = t[:, k].astype(jnp.float32)
        w = jnp.tanh(scale[:, None] * raw).astype(jnp.bfloat16)
        hot = indicator(join_class(t, k + 1))
        part = jnp.dot(w, test_hot, preferred_element_type=jnp.float32)
        per_class = lax.dot_general(
            w, hot, (((0,), (0,)), ((), ())), preferred_element_type=jnp.float32
        )
        return part, per_class

    part_m, pc_m = weigh(tr_mine)
    part_o, pc_o = weigh(tr_other)
    part = part_m + lax.ppermute(part_o, AXES, core_pairs(n))
    train_attr = cube_reduce(
        [part[o * rows:(o + 1) * rows] for o in range(8)], train_mate, n
    )
    test_part = jnp.sum((pc_m + pc_o) * test_hot.astype(jnp.float32), axis=1)
    test_attr = cube_reduce(
        [test_part[o * rows:(o + 1) * rows] for o in range(8)], test_mate, n
    )
    return (train_attr, test_attr)


def solution(mesh):
    in_specs = (
        P(AXES, None),
        P(AXES),
        P(AXES),
        P(AXES, None),
        P(AXES),
    )
    out_specs = (P(AXES, None), P(AXES))
    return jax.shard_map(local, mesh=mesh, in_specs=in_specs, out_specs=out_specs, check_vma=False)
```

```python
import jax
import jax.numpy as jnp
from jax import lax
from jax.sharding import PartitionSpec as P

NCLS = 512
PAD = 128
AXES = ("y_lo", "x_hi", "x_lo", "z_hi", "z_lo", "y_hi", "core")
CUBE = ("y_lo", "x_lo", "z_lo", "core")


def indicator(labels):
    columns = lax.broadcasted_iota(jnp.int32, (labels.shape[0], NCLS), 1)
    return (labels[:, None] == columns).astype(jnp.bfloat16)


def with_side(grads, side, first):
    rows = grads.shape[0]
    cols = lax.broadcasted_iota(jnp.int32, (rows, PAD), 1)
    extra = jnp.zeros((rows, PAD), jnp.bfloat16)
    for k, v in enumerate(side):
        extra = jnp.where(cols == first + k, v[:, None].astype(jnp.bfloat16), extra)
    return jnp.concatenate([grads, extra], axis=1)


def split_class(c):
    return (c // 32, c % 32)


def join_class(x, k):
    hi = x[:, k].astype(jnp.int32)
    lo = x[:, k + 1].astype(jnp.int32)
    return hi * 32 + lo


def coords(L):
    blk, dp = divmod(L, 16)
    yl, x = divmod(blk, 4)
    z, r = divmod(dp, 4)
    yh, c = divmod(r, 2)
    return [x, 2 * yh + yl, z], c


def lin(v, c):
    x, y, z = v
    return ((y % 2) * 4 + x) * 16 + z * 4 + (y // 2) * 2 + c


def train_mate(v):
    return v ^ 1


def test_mate(v):
    return ((((v - 1) % 4) ^ 1) + 1) % 4


def mate_pairs(n, axis, mate):
    out = []
    for L in range(n):
        v, c = coords(L)
        w = list(v)
        w[axis] = mate(v[axis])
        out.append((L, lin(w, c)))
    return out


def core_pairs(n):
    return [(L, L ^ 1) for L in range(n)]


def cube_gather(shard, mate, n):
    cols = shard.shape[1]
    tiles = cols // 128
    cut = [0, (tiles // 3) * 128, (2 * tiles // 3) * 128, cols]
    parts = []
    for p in range(3):
        order = [(p + s) % 3 for s in range(3)]
        buf = shard[:, cut[p]:cut[p + 1]]
        labs = [0]
        for a in order:
            got = lax.ppermute(buf, AXES, mate_pairs(n, a, mate))
            buf = jnp.concatenate([buf, got])
            labs = labs + [o ^ (1 << a) for o in labs]
        rows = shard.shape[0]
        parts.append({o: buf[i * rows:(i + 1) * rows] for i, o in enumerate(labs)})
    return jnp.concatenate(
        [jnp.concatenate([parts[p][o] for p in range(3)], axis=1) for o in range(8)]
    )


def cube_reduce(blocks, mate, n):
    blocks = list(blocks)
    live = list(range(8))
    for a in range(3):
        send = [o for o in live if o & (1 << a)]
        keep = [o for o in live if not o & (1 << a)]
        rows = blocks[0].shape[0]
        got = lax.ppermute(
            jnp.concatenate([blocks[o] for o in send]), AXES, mate_pairs(n, a, mate)
        )
        for i, o in enumerate(send):
            blocks[o ^ (1 << a)] = blocks[o ^ (1 << a)] + got[i * rows:(i + 1) * rows]
        live = keep
    return blocks[0]


def local(train_grads, train_scale, train_class, test_grads, test_class):
    n = 128
    k = train_grads.shape[1]
    rows = train_grads.shape[0]
    tr = with_side(train_grads, (train_scale,) + split_class(train_class), 0)
    te = with_side(test_grads, split_class(test_class), 4)
    te_all = cube_gather(te, test_mate, n)
    tr_all = lax.all_gather(tr, CUBE, axis=0, tiled=True)
    test_hot = indicator(join_class(te_all, k + 4))

    def weigh(t):
        raw = lax.dot_general(
            t, te_all, (((1,), (1,)), ((), ())), preferred_element_type=jnp.float32
        )
        scale = t[:, k].astype(jnp.float32)
        w = jnp.tanh(scale[:, None] * raw).astype(jnp.bfloat16)
        hot = indicator(join_class(t, k + 1))
        part = jnp.dot(w, test_hot, preferred_element_type=jnp.float32)
        per_class = lax.dot_general(
            w, hot, (((0,), (0,)), ((), ())), preferred_element_type=jnp.float32
        )
        return part, per_class

    part, per_class = weigh(tr_all)
    train_attr = lax.psum_scatter(part, CUBE, scatter_dimension=0, tiled=True)
    test_part = jnp.sum(per_class * test_hot.astype(jnp.float32), axis=1)
    test_attr = cube_reduce(
        [test_part[o * rows:(o + 1) * rows] for o in range(8)], test_mate, n
    )
    return (train_attr, test_attr)


def solution(mesh):
    fine = jax.sharding.Mesh(mesh.devices.reshape((2,) * 7), AXES)
    in_specs = (
        P(AXES, None),
        P(AXES),
        P(AXES),
        P(AXES, None),
        P(AXES),
    )
    out_specs = (P(AXES, None), P(AXES))
    return jax.shard_map(local, mesh=fine, in_specs=in_specs, out_specs=out_specs, check_vma=False)
```

```python
import jax
import jax.numpy as jnp
from jax import lax
from jax.sharding import PartitionSpec as P

NCLS = 512
PAD = 128
AXES = ("blk", "dp")
THREE = ((0, 1, 2), (1, 2, 0), (2, 0, 1))
TWO = ((0, 1, 2), (2, 0, 1))


def indicator(labels):
    columns = lax.broadcasted_iota(jnp.int32, (labels.shape[0], NCLS), 1)
    return (labels[:, None] == columns).astype(jnp.bfloat16)


def with_side(grads, side, first):
    rows = grads.shape[0]
    cols = lax.broadcasted_iota(jnp.int32, (rows, PAD), 1)
    extra = jnp.zeros((rows, PAD), jnp.bfloat16)
    for k, v in enumerate(side):
        extra = jnp.where(cols == first + k, v[:, None].astype(jnp.bfloat16), extra)
    return jnp.concatenate([grads, extra], axis=1)


def split_class(c):
    return (c // 32, c % 32)


def join_class(x, k):
    hi = x[:, k].astype(jnp.int32)
    lo = x[:, k + 1].astype(jnp.int32)
    return hi * 32 + lo


def coords(L):
    blk, dp = divmod(L, 16)
    yl, x = divmod(blk, 4)
    z, r = divmod(dp, 4)
    yh, c = divmod(r, 2)
    return [x, 2 * yh + yl, z], c


def lin(v, c):
    x, y, z = v
    return ((y % 2) * 4 + x) * 16 + z * 4 + (y // 2) * 2 + c


def train_mate(v):
    return v ^ 1


def test_mate(v):
    return ((((v - 1) % 4) ^ 1) + 1) % 4


def mate_pairs(n, axis, mate):
    out = []
    for L in range(n):
        v, c = coords(L)
        w = list(v)
        w[axis] = mate(v[axis])
        out.append((L, lin(w, c)))
    return out


def core_pairs(n):
    return [(L, L ^ 1) for L in range(n)]


def cube_gather(shard, mate, n, orders):
    cols = shard.shape[1]
    tiles = cols // 128
    m = len(orders)
    cut = [(tiles * p // m) * 128 for p in range(m)] + [cols]
    parts = []
    for p, order in enumerate(orders):
        buf = shard[:, cut[p]:cut[p + 1]]
        labs = [0]
        for a in order:
            got = lax.ppermute(buf, AXES, mate_pairs(n, a, mate))
            buf = jnp.concatenate([buf, got])
            labs = labs + [o ^ (1 << a) for o in labs]
        rows = shard.shape[0]
        parts.append({o: buf[i * rows:(i + 1) * rows] for i, o in enumerate(labs)})
    return jnp.concatenate(
        [jnp.concatenate([parts[p][o] for p in range(m)], axis=1) for o in range(8)]
    )


def cube_reduce(blocks, mate, n):
    blocks = list(blocks)
    live = list(range(8))
    for a in range(3):
        send = [o for o in live if o & (1 << a)]
        keep = [o for o in live if not o & (1 << a)]
        rows = blocks[0].shape[0]
        got = lax.ppermute(
            jnp.concatenate([blocks[o] for o in send]), AXES, mate_pairs(n, a, mate)
        )
        for i, o in enumerate(send):
            blocks[o ^ (1 << a)] = blocks[o ^ (1 << a)] + got[i * rows:(i + 1) * rows]
        live = keep
    return blocks[0]


def local(train_grads, train_scale, train_class, test_grads, test_class):
    n = 128
    k = train_grads.shape[1]
    rows = train_grads.shape[0]
    tr = with_side(train_grads, (train_scale,) + split_class(train_class), 0)
    te = with_side(test_grads, split_class(test_class), 4)
    te_all = cube_gather(te, test_mate, n, TWO)
    tr_mine = cube_gather(tr, train_mate, n, THREE)
    tr_other = lax.ppermute(tr_mine, AXES, core_pairs(n))
    test_hot = indicator(join_class(te_all, k + 4))

    def weigh(t):
        raw = lax.dot_general(
            t, te_all, (((1,), (1,)), ((), ())), preferred_element_type=jnp.float32
        )
        scale = t[:, k].astype(jnp.float32)
        w = jnp.tanh(scale[:, None] * raw).astype(jnp.bfloat16)
        hot = indicator(join_class(t, k + 1))
        part = jnp.dot(w, test_hot, preferred_element_type=jnp.float32)
        per_class = lax.dot_general(
            w, hot, (((0,), (0,)), ((), ())), preferred_element_type=jnp.float32
        )
        return part, per_class

    part_m, pc_m = weigh(tr_mine)
    part_o, pc_o = weigh(tr_other)
    part = part_m + lax.ppermute(part_o, AXES, core_pairs(n))
    train_attr = cube_reduce(
        [part[o * rows:(o + 1) * rows] for o in range(8)], train_mate, n
    )
    test_part = jnp.sum((pc_m + pc_o) * test_hot.astype(jnp.float32), axis=1)
    test_attr = cube_reduce(
        [test_part[o * rows:(o + 1) * rows] for o in range(8)], test_mate, n
    )
    return (train_attr, test_attr)


def solution(mesh):
    in_specs = (
        P(AXES, None),
        P(AXES),
        P(AXES),
        P(AXES, None),
        P(AXES),
    )
    out_specs = (P(AXES, None), P(AXES))
    return jax.shard_map(local, mesh=mesh, in_specs=in_specs, out_specs=out_specs, check_vma=False)
```

```python
import jax
import jax.numpy as jnp
from jax import lax
from jax.sharding import PartitionSpec as P

NCLS = 512
PAD = 128
AXES = ("y_lo", "x_hi", "x_lo", "z_hi", "z_lo", "y_hi", "core")
CUBE = ("y_lo", "x_lo", "z_lo")
THREE = ((0, 1, 2), (1, 2, 0), (2, 0, 1))
TWO = ((0, 1, 2), (2, 0, 1))


def indicator(labels):
    columns = lax.broadcasted_iota(jnp.int32, (labels.shape[0], NCLS), 1)
    return (labels[:, None] == columns).astype(jnp.bfloat16)


def with_side(grads, side, first):
    rows = grads.shape[0]
    cols = lax.broadcasted_iota(jnp.int32, (rows, PAD), 1)
    extra = jnp.zeros((rows, PAD), jnp.bfloat16)
    for k, v in enumerate(side):
        extra = jnp.where(cols == first + k, v[:, None].astype(jnp.bfloat16), extra)
    return jnp.concatenate([grads, extra], axis=1)


def split_class(c):
    return (c // 32, c % 32)


def join_class(x, k):
    hi = x[:, k].astype(jnp.int32)
    lo = x[:, k + 1].astype(jnp.int32)
    return hi * 32 + lo


def coords(L):
    blk, dp = divmod(L, 16)
    yl, x = divmod(blk, 4)
    z, r = divmod(dp, 4)
    yh, c = divmod(r, 2)
    return [x, 2 * yh + yl, z], c


def lin(v, c):
    x, y, z = v
    return ((y % 2) * 4 + x) * 16 + z * 4 + (y // 2) * 2 + c


def train_mate(v):
    return v ^ 1


def test_mate(v):
    return ((((v - 1) % 4) ^ 1) + 1) % 4


def mate_pairs(n, axis, mate):
    out = []
    for L in range(n):
        v, c = coords(L)
        w = list(v)
        w[axis] = mate(v[axis])
        out.append((L, lin(w, c)))
    return out


def core_pairs(n):
    return [(L, L ^ 1) for L in range(n)]


def column_cuts(cols, m):
    tiles = cols // 128
    return [(tiles * p // m) * 128 for p in range(m)] + [cols]


def chain(part, mate, n, order):
    rows = part.shape[0]
    buf = part
    labs = [0]
    for a in order:
        got = lax.ppermute(buf, AXES, mate_pairs(n, a, mate))
        buf = jnp.concatenate([buf, got])
        labs = labs + [o ^ (1 << a) for o in labs]
    at = {o: i for i, o in enumerate(labs)}
    return jnp.concatenate([buf[at[o] * rows:(at[o] + 1) * rows] for o in range(8)])


def cube_gather(shard, mate, n, orders):
    cut = column_cuts(shard.shape[1], len(orders))
    return jnp.concatenate(
        [chain(shard[:, cut[p]:cut[p + 1]], mate, n, order) for p, order in enumerate(orders)],
        axis=1,
    )


def sc_train_part(part):
    rows, cols = part.shape
    g = lax.all_gather(part, CUBE, axis=0, tiled=True).reshape(2, 2, 2, rows, cols)
    for axis, name in enumerate(CUBE):
        g = jnp.where(lax.axis_index(name) == 1, jnp.flip(g, axis), g)
    return g.transpose(2, 0, 1, 3, 4).reshape(8 * rows, cols)


def cube_reduce(blocks, mate, n):
    blocks = list(blocks)
    live = list(range(8))
    for a in range(3):
        send = [o for o in live if o & (1 << a)]
        keep = [o for o in live if not o & (1 << a)]
        rows = blocks[0].shape[0]
        got = lax.ppermute(
            jnp.concatenate([blocks[o] for o in send]), AXES, mate_pairs(n, a, mate)
        )
        for i, o in enumerate(send):
            blocks[o ^ (1 << a)] = blocks[o ^ (1 << a)] + got[i * rows:(i + 1) * rows]
        live = keep
    return blocks[0]


def local(train_grads, train_scale, train_class, test_grads, test_class):
    n = 128
    k = train_grads.shape[1]
    rows = train_grads.shape[0]
    tr = with_side(train_grads, (train_scale,) + split_class(train_class), 0)
    te = with_side(test_grads, split_class(test_class), 4)
    te_all = cube_gather(te, test_mate, n, THREE)
    cut = column_cuts(tr.shape[1], 3)
    tr_parts = [chain(tr[:, cut[p]:cut[p + 1]], train_mate, n, THREE[p]) for p in range(2)]
    tr_parts.append(sc_train_part(tr[:, cut[2]:]))
    tr_mine = jnp.concatenate(tr_parts, axis=1)
    tr_other = jnp.concatenate(
        [lax.ppermute(t, AXES, core_pairs(n)) for t in tr_parts], axis=1
    )
    test_hot = indicator(join_class(te_all, k + 4))

    def weigh(t):
        raw = lax.dot_general(
            t, te_all, (((1,), (1,)), ((), ())), preferred_element_type=jnp.float32
        )
        scale = t[:, k].astype(jnp.float32)
        w = jnp.tanh(scale[:, None] * raw).astype(jnp.bfloat16)
        hot = indicator(join_class(t, k + 1))
        part = jnp.dot(w, test_hot, preferred_element_type=jnp.float32)
        per_class = lax.dot_general(
            w, hot, (((0,), (0,)), ((), ())), preferred_element_type=jnp.float32
        )
        return part, per_class

    part_m, pc_m = weigh(tr_mine)
    part_o, pc_o = weigh(tr_other)
    part = part_m + lax.ppermute(part_o, AXES, core_pairs(n))
    train_attr = cube_reduce(
        [part[o * rows:(o + 1) * rows] for o in range(8)], train_mate, n
    )
    test_part = jnp.sum((pc_m + pc_o) * test_hot.astype(jnp.float32), axis=1)
    test_attr = cube_reduce(
        [test_part[o * rows:(o + 1) * rows] for o in range(8)], test_mate, n
    )
    return (train_attr, test_attr)


def solution(mesh):
    fine = jax.sharding.Mesh(mesh.devices.reshape((2,) * 7), AXES)
    in_specs = (
        P(AXES, None),
        P(AXES),
        P(AXES),
        P(AXES, None),
        P(AXES),
    )
    out_specs = (P(AXES, None), P(AXES))
    return jax.shard_map(local, mesh=fine, in_specs=in_specs, out_specs=out_specs, check_vma=False)
```

```python
import jax
import jax.numpy as jnp
from jax import lax
from jax.sharding import PartitionSpec as P

NCLS = 512
PAD = 128
AXES = ("blk", "dp")
THREE = ((0, 1, 2), (1, 2, 0), (2, 0, 1))
TWO = ((0, 1, 2), (2, 0, 1))


def indicator(labels):
    columns = lax.broadcasted_iota(jnp.int32, (labels.shape[0], NCLS), 1)
    return (labels[:, None] == columns).astype(jnp.bfloat16)


def with_side(grads, side, first):
    rows = grads.shape[0]
    cols = lax.broadcasted_iota(jnp.int32, (rows, PAD), 1)
    extra = jnp.zeros((rows, PAD), jnp.bfloat16)
    for k, v in enumerate(side):
        extra = jnp.where(cols == first + k, v[:, None].astype(jnp.bfloat16), extra)
    return jnp.concatenate([grads, extra], axis=1)


def split_class(c):
    return (c // 32, c % 32)


def join_class(x, k):
    hi = x[:, k].astype(jnp.int32)
    lo = x[:, k + 1].astype(jnp.int32)
    return hi * 32 + lo


def coords(L):
    blk, dp = divmod(L, 16)
    yl, x = divmod(blk, 4)
    z, r = divmod(dp, 4)
    yh, c = divmod(r, 2)
    return [x, 2 * yh + yl, z], c


def lin(v, c):
    x, y, z = v
    return ((y % 2) * 4 + x) * 16 + z * 4 + (y // 2) * 2 + c


def train_mate(v):
    return v ^ 1


def test_mate(v):
    return ((((v - 1) % 4) ^ 1) + 1) % 4


def mate_pairs(n, axis, mate):
    out = []
    for L in range(n):
        v, c = coords(L)
        w = list(v)
        w[axis] = mate(v[axis])
        out.append((L, lin(w, c)))
    return out


def core_pairs(n):
    return [(L, L ^ 1) for L in range(n)]


def column_cuts(cols, m):
    tiles = cols // 128
    return [(tiles * p // m) * 128 for p in range(m)] + [cols]


def chain(part, mate, n, order):
    rows = part.shape[0]
    buf = part
    labs = [0]
    for a in order:
        got = lax.ppermute(buf, AXES, mate_pairs(n, a, mate))
        buf = jnp.concatenate([buf, got])
        labs = labs + [o ^ (1 << a) for o in labs]
    at = {o: i for i, o in enumerate(labs)}
    return jnp.concatenate([buf[at[o] * rows:(at[o] + 1) * rows] for o in range(8)])


def cube_gather(shard, mate, n, orders):
    cut = column_cuts(shard.shape[1], len(orders))
    return jnp.concatenate(
        [chain(shard[:, cut[p]:cut[p + 1]], mate, n, order) for p, order in enumerate(orders)],
        axis=1,
    )


def cube_reduce(blocks, mate, n):
    blocks = list(blocks)
    live = list(range(8))
    for a in range(3):
        send = [o for o in live if o & (1 << a)]
        keep = [o for o in live if not o & (1 << a)]
        rows = blocks[0].shape[0]
        got = lax.ppermute(
            jnp.concatenate([blocks[o] for o in send]), AXES, mate_pairs(n, a, mate)
        )
        for i, o in enumerate(send):
            blocks[o ^ (1 << a)] = blocks[o ^ (1 << a)] + got[i * rows:(i + 1) * rows]
        live = keep
    return blocks[0]


def local(train_grads, train_scale, train_class, test_grads, test_class):
    n = 128
    k = train_grads.shape[1]
    rows = train_grads.shape[0]
    tr = with_side(train_grads, (train_scale,) + split_class(train_class), 0)
    te = with_side(test_grads, split_class(test_class), 4)
    cut = column_cuts(te.shape[1], 3)
    te_parts = [
        chain(te[:, cut[p]:cut[p + 1]], test_mate, n, order) for p, order in enumerate(THREE)
    ]
    te_mine = jnp.concatenate(te_parts, axis=1)
    te_other = jnp.concatenate(
        [lax.ppermute(t, AXES, core_pairs(n)) for t in te_parts], axis=1
    )
    tr_all = cube_gather(tr, train_mate, n, TWO)
    scale = tr_all[:, k].astype(jnp.float32)
    train_hot = indicator(join_class(tr_all, k + 1))

    def weigh(t):
        raw = lax.dot_general(
            tr_all, t, (((1,), (1,)), ((), ())), preferred_element_type=jnp.float32
        )
        w = jnp.tanh(scale[:, None] * raw).astype(jnp.bfloat16)
        hot = indicator(join_class(t, k + 4))
        part = jnp.dot(w, hot, preferred_element_type=jnp.float32)
        per_class = lax.dot_general(
            w, train_hot, (((0,), (0,)), ((), ())), preferred_element_type=jnp.float32
        )
        test_part = jnp.sum(per_class * hot.astype(jnp.float32), axis=1)
        return part, test_part

    part_m, tp_m = weigh(te_mine)
    part_o, tp_o = weigh(te_other)
    train_attr = cube_reduce(
        [(part_m + part_o)[o * rows:(o + 1) * rows] for o in range(8)], train_mate, n
    )
    test_part = tp_m + lax.ppermute(tp_o, AXES, core_pairs(n))
    test_attr = cube_reduce(
        [test_part[o * rows:(o + 1) * rows] for o in range(8)], test_mate, n
    )
    return (train_attr, test_attr)


def solution(mesh):
    in_specs = (
        P(AXES, None),
        P(AXES),
        P(AXES),
        P(AXES, None),
        P(AXES),
    )
    out_specs = (P(AXES, None), P(AXES))
    return jax.shard_map(local, mesh=mesh, in_specs=in_specs, out_specs=out_specs, check_vma=False)
```

```python
import jax
import jax.numpy as jnp
from jax import lax
from jax.sharding import PartitionSpec as P

NCLS = 512
PAD = 128
AXES = ("blk", "dp")
THREE = ((0, 1, 2), (1, 2, 0), (2, 0, 1))
TWO = ((0, 1, 2), (2, 0, 1))


def indicator(labels):
    columns = lax.broadcasted_iota(jnp.int32, (labels.shape[0], NCLS), 1)
    return (labels[:, None] == columns).astype(jnp.bfloat16)


def with_side(grads, side, first):
    rows, k = grads.shape
    cols = lax.broadcasted_iota(jnp.int32, (rows, PAD), 1)
    extra = jnp.zeros((rows, PAD), jnp.bfloat16)
    for j, v in enumerate(side):
        extra = jnp.where(cols == first + j, v[:, None].astype(jnp.bfloat16), extra)
    h = k // 2
    return jnp.concatenate([grads[:, :h], extra, grads[:, h:], extra], axis=1)


def split_class(c):
    return (c // 32, c % 32)


def join_class(x, k):
    hi = x[:, k].astype(jnp.int32)
    lo = x[:, k + 1].astype(jnp.int32)
    return hi * 32 + lo


def coords(L):
    blk, dp = divmod(L, 16)
    yl, x = divmod(blk, 4)
    z, r = divmod(dp, 4)
    yh, c = divmod(r, 2)
    return [x, 2 * yh + yl, z], c


def lin(v, c):
    x, y, z = v
    return ((y % 2) * 4 + x) * 16 + z * 4 + (y // 2) * 2 + c


def train_mate(v):
    return v ^ 1


def test_mate(v):
    return ((((v - 1) % 4) ^ 1) + 1) % 4


def mate_pairs(n, axis, mate):
    out = []
    for L in range(n):
        v, c = coords(L)
        w = list(v)
        w[axis] = mate(v[axis])
        out.append((L, lin(w, c)))
    return out


def core_pairs(n):
    return [(L, L ^ 1) for L in range(n)]


def column_cuts(cols, m):
    tiles = cols // 128
    return [(tiles * p // m) * 128 for p in range(m)] + [cols]


def chain(part, mate, n, order):
    rows = part.shape[0]
    buf = part
    labs = [0]
    for a in order:
        got = lax.ppermute(buf, AXES, mate_pairs(n, a, mate))
        buf = jnp.concatenate([buf, got])
        labs = labs + [o ^ (1 << a) for o in labs]
    at = {o: i for i, o in enumerate(labs)}
    return [buf[at[o] * rows:(at[o] + 1) * rows] for o in range(8)]


def half_gather(shard, mate, n, orders):
    r, cols = shard.shape
    h = cols // 2
    c = lax.axis_index(AXES) % 2
    mine = lax.dynamic_slice_in_dim(shard, c * h, h, axis=1)
    give = lax.dynamic_slice_in_dim(shard, (1 - c) * h, h, axis=1)
    unit = jnp.concatenate([mine, lax.ppermute(give, AXES, core_pairs(n))])
    cut = column_cuts(h, len(orders))
    parts = [chain(unit[:, cut[p]:cut[p + 1]], mate, n, order) for p, order in enumerate(orders)]
    blocks = [jnp.concatenate([parts[p][o] for p in range(len(orders))], axis=1) for o in range(8)]
    return jnp.concatenate([b[:r] for b in blocks] + [b[r:] for b in blocks])


def cube_gather(shard, mate, n, orders):
    cut = column_cuts(shard.shape[1], len(orders))
    return jnp.concatenate(
        [chain(shard[:, cut[p]:cut[p + 1]], mate, n, order) for p, order in enumerate(orders)],
        axis=1,
    )


def cube_reduce(blocks, mate, n):
    blocks = list(blocks)
    live = list(range(8))
    for a in range(3):
        send = [o for o in live if o & (1 << a)]
        keep = [o for o in live if not o & (1 << a)]
        rows = blocks[0].shape[0]
        got = lax.ppermute(
            jnp.concatenate([blocks[o] for o in send]), AXES, mate_pairs(n, a, mate)
        )
        for i, o in enumerate(send):
            blocks[o ^ (1 << a)] = blocks[o ^ (1 << a)] + got[i * rows:(i + 1) * rows]
        live = keep
    return blocks[0]


def local(train_grads, train_scale, train_class, test_grads, test_class):
    n = 128
    k = train_grads.shape[1]
    rows = train_grads.shape[0]
    tr = with_side(train_grads, (train_scale,) + split_class(train_class), 0)
    te = with_side(test_grads, split_class(test_class), 4)
    side = k // 2
    te_all = half_gather(te, test_mate, n, THREE)
    tr_all = half_gather(tr, train_mate, n, TWO)
    half = 8 * rows

    def partial(t):
        return lax.dot_general(
            t, te_all, (((1,), (1,)), ((), ())), preferred_element_type=jnp.float32
        )

    got = lax.ppermute(partial(tr_all[half:]), AXES, core_pairs(n))
    raw = partial(tr_all[:half]) + jnp.concatenate([got[:, half:], got[:, :half]], axis=1)
    tr_mine = tr_all[:half]
    scale = tr_mine[:, side].astype(jnp.float32)
    train_hot = indicator(join_class(tr_mine, side + 1))
    test_hot = indicator(join_class(te_all, side + 4))
    w = jnp.tanh(scale[:, None] * raw).astype(jnp.bfloat16)
    part = jnp.dot(w, test_hot, preferred_element_type=jnp.float32)
    per_class = lax.dot_general(
        w, train_hot, (((0,), (0,)), ((), ())), preferred_element_type=jnp.float32
    )
    tp = jnp.sum(per_class * test_hot.astype(jnp.float32), axis=1)
    train_attr = cube_reduce(
        [part[o * rows:(o + 1) * rows] for o in range(8)], train_mate, n
    )
    test_part = tp[:half] + lax.ppermute(tp[half:], AXES, core_pairs(n))
    test_attr = cube_reduce(
        [test_part[o * rows:(o + 1) * rows] for o in range(8)], test_mate, n
    )
    return (train_attr, test_attr)


def solution(mesh):
    in_specs = (
        P(AXES, None),
        P(AXES),
        P(AXES),
        P(AXES, None),
        P(AXES),
    )
    out_specs = (P(AXES, None), P(AXES))
    return jax.shard_map(local, mesh=mesh, in_specs=in_specs, out_specs=out_specs, check_vma=False)
```

```python
import jax
import jax.numpy as jnp
from jax import lax
from jax.sharding import PartitionSpec as P

NCLS = 512
PAD = 128
AXES = ("blk", "dp")
THREE = ((0, 1, 2), (1, 2, 0), (2, 0, 1))
TWO = ((0, 1, 2), (2, 0, 1))


def indicator(labels):
    columns = lax.broadcasted_iota(jnp.int32, (labels.shape[0], NCLS), 1)
    return (labels[:, None] == columns).astype(jnp.bfloat16)


def with_side(grads, side, first):
    rows, k = grads.shape
    cols = lax.broadcasted_iota(jnp.int32, (rows, PAD), 1)
    extra = jnp.zeros((rows, PAD), jnp.bfloat16)
    for j, v in enumerate(side):
        extra = jnp.where(cols == first + j, v[:, None].astype(jnp.bfloat16), extra)
    h = k // 2
    return jnp.concatenate([grads[:, :h], extra, grads[:, h:], extra], axis=1)


def split_class(c):
    return (c // 32, c % 32)


def join_class(x, k):
    hi = x[:, k].astype(jnp.int32)
    lo = x[:, k + 1].astype(jnp.int32)
    return hi * 32 + lo


def coords(L):
    blk, dp = divmod(L, 16)
    yl, x = divmod(blk, 4)
    z, r = divmod(dp, 4)
    yh, c = divmod(r, 2)
    return [x, 2 * yh + yl, z], c


def lin(v, c):
    x, y, z = v
    return ((y % 2) * 4 + x) * 16 + z * 4 + (y // 2) * 2 + c


def train_mate(v):
    return v ^ 1


def test_mate(v):
    return ((((v - 1) % 4) ^ 1) + 1) % 4


def mate_pairs(n, axis, mate):
    out = []
    for L in range(n):
        v, c = coords(L)
        w = list(v)
        w[axis] = mate(v[axis])
        out.append((L, lin(w, c)))
    return out


def core_pairs(n):
    return [(L, L ^ 1) for L in range(n)]


def column_cuts(cols, m):
    tiles = cols // 128
    return [(tiles * p // m) * 128 for p in range(m)] + [cols]


def chain(part, mate, n, order):
    rows = part.shape[0]
    buf = part
    labs = [0]
    for a in order:
        got = lax.ppermute(buf, AXES, mate_pairs(n, a, mate))
        buf = jnp.concatenate([buf, got])
        labs = labs + [o ^ (1 << a) for o in labs]
    at = {o: i for i, o in enumerate(labs)}
    return [buf[at[o] * rows:(at[o] + 1) * rows] for o in range(8)]


def half_gather(shard, mate, n, orders):
    r, cols = shard.shape
    h = cols // 2
    c = lax.axis_index(AXES) % 2
    mine = lax.dynamic_slice_in_dim(shard, c * h, h, axis=1)
    give = lax.dynamic_slice_in_dim(shard, (1 - c) * h, h, axis=1)
    unit = jnp.concatenate([mine, lax.ppermute(give, AXES, core_pairs(n))])
    cut = column_cuts(h, len(orders))
    parts = [chain(unit[:, cut[p]:cut[p + 1]], mate, n, order) for p, order in enumerate(orders)]
    blocks = [jnp.concatenate([parts[p][o] for p in range(len(orders))], axis=1) for o in range(8)]
    return jnp.concatenate([b[:r] for b in blocks] + [b[r:] for b in blocks])


def cube_gather(shard, mate, n, orders):
    cut = column_cuts(shard.shape[1], len(orders))
    return jnp.concatenate(
        [chain(shard[:, cut[p]:cut[p + 1]], mate, n, order) for p, order in enumerate(orders)],
        axis=1,
    )


def cube_reduce(blocks, mate, n, order=(0, 1, 2)):
    blocks = list(blocks)
    live = list(range(8))
    for a in order:
        send = [o for o in live if o & (1 << a)]
        keep = [o for o in live if not o & (1 << a)]
        rows = blocks[0].shape[0]
        got = lax.ppermute(
            jnp.concatenate([blocks[o] for o in send]), AXES, mate_pairs(n, a, mate)
        )
        for i, o in enumerate(send):
            blocks[o ^ (1 << a)] = blocks[o ^ (1 << a)] + got[i * rows:(i + 1) * rows]
        live = keep
    return blocks[0]


def cube_reduce_wide(blocks, mate, n):
    cols = blocks[0].shape[1]
    cut = [0, cols // 2, 3 * cols // 4, cols]
    return jnp.concatenate(
        [
            cube_reduce([b[:, cut[p]:cut[p + 1]] for b in blocks], mate, n, THREE[p])
            for p in range(3)
        ],
        axis=1,
    )


def local(train_grads, train_scale, train_class, test_grads, test_class):
    n = 128
    k = train_grads.shape[1]
    rows = train_grads.shape[0]
    tr = with_side(train_grads, (train_scale,) + split_class(train_class), 0)
    te = with_side(test_grads, split_class(test_class), 4)
    side = k // 2
    te_all = half_gather(te, test_mate, n, THREE)
    tr_all = half_gather(tr, train_mate, n, TWO)
    half = 8 * rows

    def partial(t):
        return lax.dot_general(
            t, te_all, (((1,), (1,)), ((), ())), preferred_element_type=jnp.float32
        )

    got = lax.ppermute(partial(tr_all[half:]), AXES, core_pairs(n))
    raw = partial(tr_all[:half]) + jnp.concatenate([got[:, half:], got[:, :half]], axis=1)
    tr_mine = tr_all[:half]
    scale = tr_mine[:, side].astype(jnp.float32)
    train_hot = indicator(join_class(tr_mine, side + 1))
    test_hot = indicator(join_class(te_all, side + 4))
    w = jnp.tanh(scale[:, None] * raw).astype(jnp.bfloat16)
    part = jnp.dot(w, test_hot, preferred_element_type=jnp.float32)
    per_class = lax.dot_general(
        w, train_hot, (((0,), (0,)), ((), ())), preferred_element_type=jnp.float32
    )
    tp = jnp.sum(per_class * test_hot.astype(jnp.float32), axis=1)
    train_attr = cube_reduce_wide(
        [part[o * rows:(o + 1) * rows] for o in range(8)], train_mate, n
    )
    test_part = tp[:half] + lax.ppermute(tp[half:], AXES, core_pairs(n))
    test_attr = cube_reduce(
        [test_part[o * rows:(o + 1) * rows] for o in range(8)], test_mate, n
    )
    return (train_attr, test_attr)


def solution(mesh):
    in_specs = (
        P(AXES, None),
        P(AXES),
        P(AXES),
        P(AXES, None),
        P(AXES),
    )
    out_specs = (P(AXES, None), P(AXES))
    return jax.shard_map(local, mesh=mesh, in_specs=in_specs, out_specs=out_specs, check_vma=False)
```

```python
import jax
import jax.numpy as jnp
from jax import lax
from jax.sharding import PartitionSpec as P

NCLS = 512
PAD = 128
AXES = ("y_lo", "x_hi", "x_lo", "z_hi", "z_lo", "y_hi", "core")
CUBE = ("x_lo", "y_lo", "z_lo")
THREE = ((0, 1, 2), (1, 2, 0), (2, 0, 1))
TWO = ((0, 1, 2), (2, 0, 1))


def indicator(labels):
    columns = lax.broadcasted_iota(jnp.int32, (labels.shape[0], NCLS), 1)
    return (labels[:, None] == columns).astype(jnp.bfloat16)


def with_side(grads, side, first):
    rows, k = grads.shape
    cols = lax.broadcasted_iota(jnp.int32, (rows, PAD), 1)
    extra = jnp.zeros((rows, PAD), jnp.bfloat16)
    for j, v in enumerate(side):
        extra = jnp.where(cols == first + j, v[:, None].astype(jnp.bfloat16), extra)
    h = k // 2
    return jnp.concatenate([grads[:, :h], extra, grads[:, h:], extra], axis=1)


def split_class(c):
    return (c // 32, c % 32)


def join_class(x, k):
    hi = x[:, k].astype(jnp.int32)
    lo = x[:, k + 1].astype(jnp.int32)
    return hi * 32 + lo


def coords(L):
    blk, dp = divmod(L, 16)
    yl, x = divmod(blk, 4)
    z, r = divmod(dp, 4)
    yh, c = divmod(r, 2)
    return [x, 2 * yh + yl, z], c


def lin(v, c):
    x, y, z = v
    return ((y % 2) * 4 + x) * 16 + z * 4 + (y // 2) * 2 + c


def train_mate(v):
    return v ^ 1


def test_mate(v):
    return ((((v - 1) % 4) ^ 1) + 1) % 4


def mate_pairs(n, axis, mate):
    out = []
    for L in range(n):
        v, c = coords(L)
        w = list(v)
        w[axis] = mate(v[axis])
        out.append((L, lin(w, c)))
    return out


def core_pairs(n):
    return [(L, L ^ 1) for L in range(n)]


def column_cuts(cols, m):
    tiles = cols // 128
    return [(tiles * p // m) * 128 for p in range(m)] + [cols]


def chain(part, mate, n, order):
    rows = part.shape[0]
    buf = part
    labs = [0]
    for a in order:
        got = lax.ppermute(buf, AXES, mate_pairs(n, a, mate))
        buf = jnp.concatenate([buf, got])
        labs = labs + [o ^ (1 << a) for o in labs]
    at = {o: i for i, o in enumerate(labs)}
    return [buf[at[o] * rows:(at[o] + 1) * rows] for o in range(8)]


def a2a_chain(part, order):
    rows, cols = part.shape
    buf = part[None]
    for a in order:
        buf = lax.all_to_all(jnp.stack([buf, buf]), CUBE[a], 0, 0, tiled=False)
    for d, a in enumerate(reversed(order)):
        buf = jnp.where(lax.axis_index(CUBE[a]) == 1, jnp.flip(buf, d), buf)
    perm = [list(reversed(order)).index(a) for a in (2, 1, 0)]
    buf = buf.reshape(2, 2, 2, rows, cols).transpose(perm + [3, 4])
    return [buf.reshape(8, rows, cols)[o] for o in range(8)]


def half_gather(shard, mate, n, orders, a2a=0):
    r, cols = shard.shape
    h = cols // 2
    c = lax.axis_index(AXES) % 2
    mine = lax.dynamic_slice_in_dim(shard, c * h, h, axis=1)
    give = lax.dynamic_slice_in_dim(shard, (1 - c) * h, h, axis=1)
    unit = jnp.concatenate([mine, lax.ppermute(give, AXES, core_pairs(n))])
    m = len(orders) + a2a
    cut = column_cuts(h, m)
    parts = [chain(unit[:, cut[p]:cut[p + 1]], mate, n, order) for p, order in enumerate(orders)]
    for p in range(len(orders), m):
        parts.append(a2a_chain(unit[:, cut[p]:cut[p + 1]], THREE[p]))
    blocks = [jnp.concatenate([parts[p][o] for p in range(m)], axis=1) for o in range(8)]
    return jnp.concatenate([b[:r] for b in blocks] + [b[r:] for b in blocks])


def cube_reduce(blocks, mate, n):
    blocks = list(blocks)
    live = list(range(8))
    for a in range(3):
        send = [o for o in live if o & (1 << a)]
        keep = [o for o in live if not o & (1 << a)]
        rows = blocks[0].shape[0]
        got = lax.ppermute(
            jnp.concatenate([blocks[o] for o in send]), AXES, mate_pairs(n, a, mate)
        )
        for i, o in enumerate(send):
            blocks[o ^ (1 << a)] = blocks[o ^ (1 << a)] + got[i * rows:(i + 1) * rows]
        live = keep
    return blocks[0]


def local(train_grads, train_scale, train_class, test_grads, test_class):
    n = 128
    k = train_grads.shape[1]
    rows = train_grads.shape[0]
    tr = with_side(train_grads, (train_scale,) + split_class(train_class), 0)
    te = with_side(test_grads, split_class(test_class), 4)
    side = k // 2
    te_all = half_gather(te, test_mate, n, THREE)
    tr_all = half_gather(tr, train_mate, n, TWO, a2a=1)
    half = 8 * rows

    def partial(t):
        return lax.dot_general(
            t, te_all, (((1,), (1,)), ((), ())), preferred_element_type=jnp.float32
        )

    got = lax.ppermute(partial(tr_all[half:]), AXES, core_pairs(n))
    raw = partial(tr_all[:half]) + jnp.concatenate([got[:, half:], got[:, :half]], axis=1)
    tr_mine = tr_all[:half]
    scale = tr_mine[:, side].astype(jnp.float32)
    train_hot = indicator(join_class(tr_mine, side + 1))
    test_hot = indicator(join_class(te_all, side + 4))
    w = jnp.tanh(scale[:, None] * raw).astype(jnp.bfloat16)
    part = jnp.dot(w, test_hot, preferred_element_type=jnp.float32)
    per_class = lax.dot_general(
        w, train_hot, (((0,), (0,)), ((), ())), preferred_element_type=jnp.float32
    )
    tp = jnp.sum(per_class * test_hot.astype(jnp.float32), axis=1)
    train_attr = cube_reduce(
        [part[o * rows:(o + 1) * rows] for o in range(8)], train_mate, n
    )
    test_part = tp[:half] + lax.ppermute(tp[half:], AXES, core_pairs(n))
    test_attr = cube_reduce(
        [test_part[o * rows:(o + 1) * rows] for o in range(8)], test_mate, n
    )
    return (train_attr, test_attr)


def solution(mesh):
    fine = jax.sharding.Mesh(mesh.devices.reshape((2,) * 7), AXES)
    in_specs = (
        P(AXES, None),
        P(AXES),
        P(AXES),
        P(AXES, None),
        P(AXES),
    )
    out_specs = (P(AXES, None), P(AXES))
    return jax.shard_map(local, mesh=fine, in_specs=in_specs, out_specs=out_specs, check_vma=False)
```

```python
import jax
import jax.numpy as jnp
from jax import lax
from jax.sharding import PartitionSpec as P

NCLS = 512
PAD = 128
AXES = ("blk", "dp")
THREE = ((0, 1, 2), (1, 2, 0), (2, 0, 1))
TWO = ((0, 1, 2), (2, 0, 1))


def indicator(labels):
    columns = lax.broadcasted_iota(jnp.int32, (labels.shape[0], NCLS), 1)
    return (labels[:, None] == columns).astype(jnp.bfloat16)


def with_side(grads, side, first):
    rows, k = grads.shape
    cols = lax.broadcasted_iota(jnp.int32, (rows, PAD), 1)
    extra = jnp.zeros((rows, PAD), jnp.bfloat16)
    for j, v in enumerate(side):
        extra = jnp.where(cols == first + j, v[:, None].astype(jnp.bfloat16), extra)
    h = k // 2
    return jnp.concatenate([grads[:, :h], extra, grads[:, h:], extra], axis=1)


def split_class(c):
    return (c // 32, c % 32)


def join_class(x, k):
    hi = x[:, k].astype(jnp.int32)
    lo = x[:, k + 1].astype(jnp.int32)
    return hi * 32 + lo


def coords(L):
    blk, dp = divmod(L, 16)
    yl, x = divmod(blk, 4)
    z, r = divmod(dp, 4)
    yh, c = divmod(r, 2)
    return [x, 2 * yh + yl, z], c


def lin(v, c):
    x, y, z = v
    return ((y % 2) * 4 + x) * 16 + z * 4 + (y // 2) * 2 + c


def train_mate(v):
    return v ^ 1


def test_mate(v):
    return ((((v - 1) % 4) ^ 1) + 1) % 4


def mate_pairs(n, axis, mate):
    out = []
    for L in range(n):
        v, c = coords(L)
        w = list(v)
        w[axis] = mate(v[axis])
        out.append((L, lin(w, c)))
    return out


def core_pairs(n):
    return [(L, L ^ 1) for L in range(n)]


def column_cuts(cols, m):
    tiles = cols // 128
    return [(tiles * p // m) * 128 for p in range(m)] + [cols]


def chain(part, mate, n, order):
    rows = part.shape[0]
    buf = part
    labs = [0]
    for a in order:
        got = lax.ppermute(buf, AXES, mate_pairs(n, a, mate))
        buf = jnp.concatenate([buf, got])
        labs = labs + [o ^ (1 << a) for o in labs]
    at = {o: i for i, o in enumerate(labs)}
    return [buf[at[o] * rows:(at[o] + 1) * rows] for o in range(8)]


def half_unit(shard, n):
    h = shard.shape[1] // 2
    c = lax.axis_index(AXES) % 2
    mine = lax.dynamic_slice_in_dim(shard, c * h, h, axis=1)
    give = lax.dynamic_slice_in_dim(shard, (1 - c) * h, h, axis=1)
    return jnp.concatenate([mine, lax.ppermute(give, AXES, core_pairs(n))])


def half_gather(unit, mate, n, orders):
    r = unit.shape[0] // 2
    cut = column_cuts(unit.shape[1], len(orders))
    parts = [chain(unit[:, cut[p]:cut[p + 1]], mate, n, order) for p, order in enumerate(orders)]
    blocks = [jnp.concatenate([parts[p][o] for p in range(len(orders))], axis=1) for o in range(8)]
    return jnp.concatenate([b[:r] for b in blocks] + [b[r:] for b in blocks])


def cube_reduce(blocks, mate, n):
    blocks = list(blocks)
    live = list(range(8))
    for a in range(3):
        send = [o for o in live if o & (1 << a)]
        keep = [o for o in live if not o & (1 << a)]
        rows = blocks[0].shape[0]
        got = lax.ppermute(
            jnp.concatenate([blocks[o] for o in send]), AXES, mate_pairs(n, a, mate)
        )
        for i, o in enumerate(send):
            blocks[o ^ (1 << a)] = blocks[o ^ (1 << a)] + got[i * rows:(i + 1) * rows]
        live = keep
    return blocks[0]


def local(train_grads, train_scale, train_class, test_grads, test_class):
    n = 128
    k = train_grads.shape[1]
    rows = train_grads.shape[0]
    tr = with_side(train_grads, (train_scale,) + split_class(train_class), 0)
    te = with_side(test_grads, split_class(test_class), 4)
    side = k // 2
    tr_unit, te_unit = lax.optimization_barrier((half_unit(tr, n), half_unit(te, n)))
    tr_all = half_gather(tr_unit, train_mate, n, TWO)
    te_all = half_gather(te_unit, test_mate, n, THREE)
    half = 8 * rows

    def partial(t):
        return lax.dot_general(
            t, te_all, (((1,), (1,)), ((), ())), preferred_element_type=jnp.float32
        )

    got = lax.ppermute(partial(tr_all[half:]), AXES, core_pairs(n))
    raw = partial(tr_all[:half]) + jnp.concatenate([got[:, half:], got[:, :half]], axis=1)
    tr_mine = tr_all[:half]
    scale = tr_mine[:, side].astype(jnp.float32)
    train_hot = indicator(join_class(tr_mine, side + 1))
    test_hot = indicator(join_class(te_all, side + 4))
    w = jnp.tanh(scale[:, None] * raw).astype(jnp.bfloat16)
    part = jnp.dot(w, test_hot, preferred_element_type=jnp.float32)
    per_class = lax.dot_general(
        w, train_hot, (((0,), (0,)), ((), ())), preferred_element_type=jnp.float32
    )
    tp = jnp.sum(per_class * test_hot.astype(jnp.float32), axis=1)
    train_attr = cube_reduce(
        [part[o * rows:(o + 1) * rows] for o in range(8)], train_mate, n
    )
    test_part = tp[:half] + lax.ppermute(tp[half:], AXES, core_pairs(n))
    test_attr = cube_reduce(
        [test_part[o * rows:(o + 1) * rows] for o in range(8)], test_mate, n
    )
    return (train_attr, test_attr)


def solution(mesh):
    in_specs = (
        P(AXES, None),
        P(AXES),
        P(AXES),
        P(AXES, None),
        P(AXES),
    )
    out_specs = (P(AXES, None), P(AXES))
    return jax.shard_map(local, mesh=mesh, in_specs=in_specs, out_specs=out_specs, check_vma=False)
```

```python
import jax
import jax.numpy as jnp
from jax import lax
from jax.sharding import PartitionSpec as P

NCLS = 512
PAD = 128
AXES = ("blk", "dp")
THREE = ((0, 1, 2), (1, 2, 0), (2, 0, 1))
TWO = ((0, 1, 2), (2, 0, 1))


def indicator(labels):
    columns = lax.broadcasted_iota(jnp.int32, (labels.shape[0], NCLS), 1)
    return (labels[:, None] == columns).astype(jnp.bfloat16)


def with_side(grads, side, first):
    rows, k = grads.shape
    cols = lax.broadcasted_iota(jnp.int32, (rows, PAD), 1)
    extra = jnp.zeros((rows, PAD), jnp.bfloat16)
    for j, v in enumerate(side):
        extra = jnp.where(cols == first + j, v[:, None].astype(jnp.bfloat16), extra)
    h = k // 2
    return jnp.concatenate([grads[:, :h], extra, grads[:, h:], extra], axis=1)


def split_class(c):
    return (c // 32, c % 32)


def join_class(x, k):
    hi = x[:, k].astype(jnp.int32)
    lo = x[:, k + 1].astype(jnp.int32)
    return hi * 32 + lo


def coords(L):
    blk, dp = divmod(L, 16)
    yl, x = divmod(blk, 4)
    z, r = divmod(dp, 4)
    yh, c = divmod(r, 2)
    return [x, 2 * yh + yl, z], c


def lin(v, c):
    x, y, z = v
    return ((y % 2) * 4 + x) * 16 + z * 4 + (y // 2) * 2 + c


def train_mate(v):
    return v ^ 1


def test_mate(v):
    return ((((v - 1) % 4) ^ 1) + 1) % 4


def mate_pairs(n, axis, mate):
    out = []
    for L in range(n):
        v, c = coords(L)
        w = list(v)
        w[axis] = mate(v[axis])
        out.append((L, lin(w, c)))
    return out


def core_pairs(n):
    return [(L, L ^ 1) for L in range(n)]


def column_cuts(cols, m):
    tiles = cols // 128
    return [(tiles * p // m) * 128 for p in range(m)] + [cols]


def chain(part, mate, n, order):
    rows = part.shape[0]
    buf = part
    labs = [0]
    for a in order:
        got = lax.ppermute(buf, AXES, mate_pairs(n, a, mate))
        buf = jnp.concatenate([buf, got])
        labs = labs + [o ^ (1 << a) for o in labs]
    at = {o: i for i, o in enumerate(labs)}
    return [buf[at[o] * rows:(at[o] + 1) * rows] for o in range(8)]


def half_gather(shard, mate, n, orders):
    r, cols = shard.shape
    h = cols // 2
    c = lax.axis_index(AXES) % 2
    mine = lax.dynamic_slice_in_dim(shard, c * h, h, axis=1)
    give = lax.dynamic_slice_in_dim(shard, (1 - c) * h, h, axis=1)
    unit = jnp.concatenate([mine, lax.ppermute(give, AXES, core_pairs(n))])
    cut = column_cuts(h, len(orders))
    parts = [chain(unit[:, cut[p]:cut[p + 1]], mate, n, order) for p, order in enumerate(orders)]
    blocks = [jnp.concatenate([parts[p][o] for p in range(len(orders))], axis=1) for o in range(8)]
    return jnp.concatenate([b[:r] for b in blocks] + [b[r:] for b in blocks])


def cube_gather(shard, mate, n, orders):
    cut = column_cuts(shard.shape[1], len(orders))
    return jnp.concatenate(
        [chain(shard[:, cut[p]:cut[p + 1]], mate, n, order) for p, order in enumerate(orders)],
        axis=1,
    )


def cube_reduce(blocks, mate, n):
    blocks = list(blocks)
    live = list(range(8))
    for a in range(3):
        send = [o for o in live if o & (1 << a)]
        keep = [o for o in live if not o & (1 << a)]
        rows = blocks[0].shape[0]
        got = lax.ppermute(
            jnp.concatenate([blocks[o] for o in send]), AXES, mate_pairs(n, a, mate)
        )
        for i, o in enumerate(send):
            blocks[o ^ (1 << a)] = blocks[o ^ (1 << a)] + got[i * rows:(i + 1) * rows]
        live = keep
    return blocks[0]


def local(train_grads, train_scale, train_class, test_grads, test_class):
    n = 128
    k = train_grads.shape[1]
    rows = train_grads.shape[0]
    tr = with_side(train_grads, (train_scale,) + split_class(train_class), 0)
    te = with_side(test_grads, split_class(test_class), 4)
    side = k // 2
    te_all = half_gather(te, test_mate, n, THREE)
    tr_all = half_gather(tr, train_mate, n, TWO)
    half = 8 * rows

    def partial(t):
        return lax.dot_general(
            t, te_all, (((1,), (1,)), ((), ())), preferred_element_type=jnp.float32
        )

    got = lax.ppermute(partial(tr_all[half:]), AXES, core_pairs(n))
    own = lax.optimization_barrier(partial(tr_all[:half]))
    raw = own + jnp.concatenate([got[:, half:], got[:, :half]], axis=1)
    tr_mine = tr_all[:half]
    scale = tr_mine[:, side].astype(jnp.float32)
    train_hot = indicator(join_class(tr_mine, side + 1))
    test_hot = indicator(join_class(te_all, side + 4))
    w = jnp.tanh(scale[:, None] * raw).astype(jnp.bfloat16)
    part = jnp.dot(w, test_hot, preferred_element_type=jnp.float32)
    per_class = lax.dot_general(
        w, train_hot, (((0,), (0,)), ((), ())), preferred_element_type=jnp.float32
    )
    tp = jnp.sum(per_class * test_hot.astype(jnp.float32), axis=1)
    train_attr = cube_reduce(
        [part[o * rows:(o + 1) * rows] for o in range(8)], train_mate, n
    )
    test_part = tp[:half] + lax.ppermute(tp[half:], AXES, core_pairs(n))
    test_attr = cube_reduce(
        [test_part[o * rows:(o + 1) * rows] for o in range(8)], test_mate, n
    )
    return (train_attr, test_attr)


def solution(mesh):
    in_specs = (
        P(AXES, None),
        P(AXES),
        P(AXES),
        P(AXES, None),
        P(AXES),
    )
    out_specs = (P(AXES, None), P(AXES))
    return jax.shard_map(local, mesh=mesh, in_specs=in_specs, out_specs=out_specs, check_vma=False)
```

```python
import jax
import jax.numpy as jnp
from jax import lax
from jax.sharding import PartitionSpec as P

NCLS = 512
PAD = 128
AXES = ("blk", "dp")
THREE = ((0, 1, 2), (1, 2, 0), (2, 0, 1))
TWO = ((0, 1, 2), (2, 0, 1))


def indicator(labels):
    columns = lax.broadcasted_iota(jnp.int32, (labels.shape[0], NCLS), 1)
    return (labels[:, None] == columns).astype(jnp.bfloat16)


def with_side(grads, side, first):
    rows, k = grads.shape
    cols = lax.broadcasted_iota(jnp.int32, (rows, PAD), 1)
    extra = jnp.zeros((rows, PAD), jnp.bfloat16)
    for j, v in enumerate(side):
        extra = jnp.where(cols == first + j, v[:, None].astype(jnp.bfloat16), extra)
    h = k // 2
    return jnp.concatenate([grads[:, :h], extra, grads[:, h:], extra], axis=1)


def split_class(c):
    return (c // 32, c % 32)


def join_class(x, k):
    hi = x[:, k].astype(jnp.int32)
    lo = x[:, k + 1].astype(jnp.int32)
    return hi * 32 + lo


def coords(L):
    blk, dp = divmod(L, 16)
    yl, x = divmod(blk, 4)
    z, r = divmod(dp, 4)
    yh, c = divmod(r, 2)
    return [x, 2 * yh + yl, z], c


def lin(v, c):
    x, y, z = v
    return ((y % 2) * 4 + x) * 16 + z * 4 + (y // 2) * 2 + c


def train_mate(v):
    return v ^ 1


def test_mate(v):
    return ((((v - 1) % 4) ^ 1) + 1) % 4


def mate_pairs(n, axis, mate):
    out = []
    for L in range(n):
        v, c = coords(L)
        w = list(v)
        w[axis] = mate(v[axis])
        out.append((L, lin(w, c)))
    return out


def core_pairs(n):
    return [(L, L ^ 1) for L in range(n)]


def column_cuts(cols, m):
    tiles = cols // 128
    return [(tiles * p // m) * 128 for p in range(m)] + [cols]


def chain(part, mate, n, order):
    rows = part.shape[0]
    buf = part
    labs = [0]
    for a in order:
        got = lax.ppermute(buf, AXES, mate_pairs(n, a, mate))
        buf = jnp.concatenate([buf, got])
        labs = labs + [o ^ (1 << a) for o in labs]
    at = {o: i for i, o in enumerate(labs)}
    return [buf[at[o] * rows:(at[o] + 1) * rows] for o in range(8)]


def half_gather(shard, mate, n, orders):
    r, cols = shard.shape
    h = cols // 2
    c = lax.axis_index(AXES) % 2
    mine = lax.dynamic_slice_in_dim(shard, c * h, h, axis=1)
    give = lax.dynamic_slice_in_dim(shard, (1 - c) * h, h, axis=1)
    unit = jnp.concatenate([mine, lax.ppermute(give, AXES, core_pairs(n))])
    cut = column_cuts(h, len(orders))
    parts = [chain(unit[:, cut[p]:cut[p + 1]], mate, n, order) for p, order in enumerate(orders)]
    blocks = [jnp.concatenate([parts[p][o] for p in range(len(orders))], axis=1) for o in range(8)]
    return jnp.concatenate([b[:r] for b in blocks] + [b[r:] for b in blocks])


def cube_gather(shard, mate, n, orders):
    cut = column_cuts(shard.shape[1], len(orders))
    return jnp.concatenate(
        [chain(shard[:, cut[p]:cut[p + 1]], mate, n, order) for p, order in enumerate(orders)],
        axis=1,
    )


HALVE = ((0, 1, 2), (1, 2, 0))


def halve_pairs(n, step, mate):
    out = []
    for L in range(n):
        v, c = coords(L)
        a = HALVE[c][step]
        w = list(v)
        w[a] = mate(v[a])
        out.append((L, lin(w, c)))
    return out


def cube_reduce(blocks, mate, n):
    def phys(q, order):
        return sum(((q >> s) & 1) << order[s] for s in range(3))

    stacked = jnp.stack(blocks)
    c = lax.axis_index(AXES) % 2
    stacked = jnp.where(c == 0, stacked, stacked[jnp.array([phys(q, HALVE[1]) for q in range(8)])])
    blocks = [stacked[q] for q in range(8)]
    live = list(range(8))
    for step in range(3):
        send = [q for q in live if q & (1 << step)]
        keep = [q for q in live if not q & (1 << step)]
        rows = blocks[0].shape[0]
        got = lax.ppermute(
            jnp.concatenate([blocks[q] for q in send]), AXES, halve_pairs(n, step, mate)
        )
        for i, q in enumerate(send):
            blocks[q ^ (1 << step)] = blocks[q ^ (1 << step)] + got[i * rows:(i + 1) * rows]
        live = keep
    return blocks[0]


def local(train_grads, train_scale, train_class, test_grads, test_class):
    n = 128
    k = train_grads.shape[1]
    rows = train_grads.shape[0]
    tr = with_side(train_grads, (train_scale,) + split_class(train_class), 0)
    te = with_side(test_grads, split_class(test_class), 4)
    side = k // 2
    te_all = half_gather(te, test_mate, n, THREE)
    tr_all = half_gather(tr, train_mate, n, TWO)
    half = 8 * rows

    def partial(t):
        return lax.dot_general(
            t, te_all, (((1,), (1,)), ((), ())), preferred_element_type=jnp.float32
        )

    got = lax.ppermute(partial(tr_all[half:]), AXES, core_pairs(n))
    own = lax.optimization_barrier(partial(tr_all[:half]))
    raw = own + jnp.concatenate([got[:, half:], got[:, :half]], axis=1)
    tr_mine = tr_all[:half]
    scale = tr_mine[:, side].astype(jnp.float32)
    train_hot = indicator(join_class(tr_mine, side + 1))
    test_hot = indicator(join_class(te_all, side + 4))
    w = jnp.tanh(scale[:, None] * raw).astype(jnp.bfloat16)
    part = jnp.dot(w, test_hot, preferred_element_type=jnp.float32)
    per_class = lax.dot_general(
        w, train_hot, (((0,), (0,)), ((), ())), preferred_element_type=jnp.float32
    )
    tp = jnp.sum(per_class * test_hot.astype(jnp.float32), axis=1)
    train_attr = cube_reduce(
        [part[o * rows:(o + 1) * rows] for o in range(8)], train_mate, n
    )
    test_part = tp[:half] + lax.ppermute(tp[half:], AXES, core_pairs(n))
    test_attr = cube_reduce(
        [test_part[o * rows:(o + 1) * rows] for o in range(8)], test_mate, n
    )
    return (train_attr, test_attr)


def solution(mesh):
    in_specs = (
        P(AXES, None),
        P(AXES),
        P(AXES),
        P(AXES, None),
        P(AXES),
    )
    out_specs = (P(AXES, None), P(AXES))
    return jax.shard_map(local, mesh=mesh, in_specs=in_specs, out_specs=out_specs, check_vma=False)
```

```python
import jax
import jax.numpy as jnp
from jax import lax
from jax.sharding import PartitionSpec as P

NCLS = 512
PAD = 128
AXES = ("blk", "dp")
THREE = ((0, 1, 2), (1, 2, 0), (2, 0, 1))
TWO = ((0, 1, 2), (2, 0, 1))


def indicator(labels):
    columns = lax.broadcasted_iota(jnp.int32, (labels.shape[0], NCLS), 1)
    return (labels[:, None] == columns).astype(jnp.bfloat16)


def with_side(grads, side, first):
    rows, k = grads.shape
    cols = lax.broadcasted_iota(jnp.int32, (rows, PAD), 1)
    extra = jnp.zeros((rows, PAD), jnp.bfloat16)
    for j, v in enumerate(side):
        extra = jnp.where(cols == first + j, v[:, None].astype(jnp.bfloat16), extra)
    h = k // 2
    return jnp.concatenate([grads[:, :h], extra, grads[:, h:], extra], axis=1)


def split_class(c):
    return (c // 32, c % 32)


def join_class(x, k):
    hi = x[:, k].astype(jnp.int32)
    lo = x[:, k + 1].astype(jnp.int32)
    return hi * 32 + lo


def coords(L):
    blk, dp = divmod(L, 16)
    yl, x = divmod(blk, 4)
    z, r = divmod(dp, 4)
    yh, c = divmod(r, 2)
    return [x, 2 * yh + yl, z], c


def lin(v, c):
    x, y, z = v
    return ((y % 2) * 4 + x) * 16 + z * 4 + (y // 2) * 2 + c


def train_mate(v):
    return v ^ 1


def test_mate(v):
    return ((((v - 1) % 4) ^ 1) + 1) % 4


def mate_pairs(n, axis, mate):
    out = []
    for L in range(n):
        v, c = coords(L)
        w = list(v)
        w[axis] = mate(v[axis])
        out.append((L, lin(w, c)))
    return out


def core_pairs(n):
    return [(L, L ^ 1) for L in range(n)]


def column_cuts(cols, m):
    tiles = cols // 128
    return [(tiles * p // m) * 128 for p in range(m)] + [cols]


def chain(part, mate, n, order):
    rows = part.shape[0]
    buf = part
    labs = [0]
    for a in order:
        got = lax.ppermute(buf, AXES, mate_pairs(n, a, mate))
        buf = jnp.concatenate([buf, got])
        labs = labs + [o ^ (1 << a) for o in labs]
    at = {o: i for i, o in enumerate(labs)}
    return [buf[at[o] * rows:(at[o] + 1) * rows] for o in range(8)]


def half_gather(shard, mate, n, orders):
    r, cols = shard.shape
    h = cols // 2
    c = lax.axis_index(AXES) % 2
    mine = lax.dynamic_slice_in_dim(shard, c * h, h, axis=1)
    give = lax.dynamic_slice_in_dim(shard, (1 - c) * h, h, axis=1)
    unit = jnp.concatenate([mine, lax.ppermute(give, AXES, core_pairs(n))])
    cut = column_cuts(h, len(orders))
    parts = [chain(unit[:, cut[p]:cut[p + 1]], mate, n, order) for p, order in enumerate(orders)]
    blocks = [jnp.concatenate([parts[p][o] for p in range(len(orders))], axis=1) for o in range(8)]
    return jnp.concatenate([b[:r] for b in blocks] + [b[r:] for b in blocks])


def cube_gather(shard, mate, n, orders):
    cut = column_cuts(shard.shape[1], len(orders))
    return jnp.concatenate(
        [chain(shard[:, cut[p]:cut[p + 1]], mate, n, order) for p, order in enumerate(orders)],
        axis=1,
    )


def cube_reduce(blocks, mate, n):
    blocks = list(blocks)
    live = list(range(8))
    for a in range(3):
        send = [o for o in live if o & (1 << a)]
        keep = [o for o in live if not o & (1 << a)]
        rows = blocks[0].shape[0]
        got = lax.ppermute(
            jnp.concatenate([blocks[o] for o in send]), AXES, mate_pairs(n, a, mate)
        )
        for i, o in enumerate(send):
            blocks[o ^ (1 << a)] = blocks[o ^ (1 << a)] + got[i * rows:(i + 1) * rows]
        live = keep
    return blocks[0]


HALVE = ((0, 1, 2), (1, 2, 0))


def halve_pairs(n, step, mate):
    out = []
    for L in range(n):
        v, c = coords(L)
        a = HALVE[c][step]
        w = list(v)
        w[a] = mate(v[a])
        out.append((L, lin(w, c)))
    return out


def cube_reduce_split(blocks, mate, n):
    def phys(q, order):
        return sum(((q >> s) & 1) << order[s] for s in range(3))

    c = lax.axis_index(AXES) % 2
    blocks = [jnp.where(c == 0, blocks[phys(q, HALVE[0])], blocks[phys(q, HALVE[1])]) for q in range(8)]
    live = list(range(8))
    for step in range(3):
        send = [q for q in live if q & (1 << step)]
        keep = [q for q in live if not q & (1 << step)]
        rows = blocks[0].shape[0]
        got = lax.ppermute(
            jnp.concatenate([blocks[q] for q in send]), AXES, halve_pairs(n, step, mate)
        )
        for i, q in enumerate(send):
            blocks[q ^ (1 << step)] = blocks[q ^ (1 << step)] + got[i * rows:(i + 1) * rows]
        live = keep
    return blocks[0]


def local(train_grads, train_scale, train_class, test_grads, test_class):
    n = 128
    k = train_grads.shape[1]
    rows = train_grads.shape[0]
    tr = with_side(train_grads, (train_scale,) + split_class(train_class), 0)
    te = with_side(test_grads, split_class(test_class), 4)
    side = k // 2
    te_all = half_gather(te, test_mate, n, THREE)
    tr_all = half_gather(tr, train_mate, n, TWO)
    half = 8 * rows

    def partial(t):
        return lax.dot_general(
            t, te_all, (((1,), (1,)), ((), ())), preferred_element_type=jnp.float32
        )

    got = lax.ppermute(partial(tr_all[half:]), AXES, core_pairs(n))
    own = lax.optimization_barrier(partial(tr_all[:half]))
    raw = own + jnp.concatenate([got[:, half:], got[:, :half]], axis=1)
    tr_mine = tr_all[:half]
    scale = tr_mine[:, side].astype(jnp.float32)
    train_hot = indicator(join_class(tr_mine, side + 1))
    test_hot = indicator(join_class(te_all, side + 4))
    w = jnp.tanh(scale[:, None] * raw).astype(jnp.bfloat16)
    part = jnp.dot(w, test_hot, preferred_element_type=jnp.float32)
    per_class = lax.dot_general(
        w, train_hot, (((0,), (0,)), ((), ())), preferred_element_type=jnp.float32
    )
    tp = jnp.sum(per_class * test_hot.astype(jnp.float32), axis=1)
    train_attr = cube_reduce_split(
        [part[o * rows:(o + 1) * rows] for o in range(8)], train_mate, n
    )
    test_part = tp[:half] + lax.ppermute(tp[half:], AXES, core_pairs(n))
    test_attr = cube_reduce(
        [test_part[o * rows:(o + 1) * rows] for o in range(8)], test_mate, n
    )
    return (train_attr, test_attr)


def solution(mesh):
    in_specs = (
        P(AXES, None),
        P(AXES),
        P(AXES),
        P(AXES, None),
        P(AXES),
    )
    out_specs = (P(AXES, None), P(AXES))
    return jax.shard_map(local, mesh=mesh, in_specs=in_specs, out_specs=out_specs, check_vma=False)
```

```python
import jax
import jax.numpy as jnp
from jax import lax
from jax.sharding import PartitionSpec as P

NCLS = 512
PAD = 128
AXES = ("blk", "dp")
THREE = ((0, 1, 2), (1, 2, 0), (2, 0, 1))
TWO = ((0, 1, 2), (2, 0, 1))


def indicator(labels):
    columns = lax.broadcasted_iota(jnp.int32, (labels.shape[0], NCLS), 1)
    return (labels[:, None] == columns).astype(jnp.bfloat16)


def with_side(grads, side, first):
    rows, k = grads.shape
    cols = lax.broadcasted_iota(jnp.int32, (rows, PAD), 1)
    extra = jnp.zeros((rows, PAD), jnp.bfloat16)
    for j, v in enumerate(side):
        extra = jnp.where(cols == first + j, v[:, None].astype(jnp.bfloat16), extra)
    h = k // 2
    return jnp.concatenate([grads[:, :h], extra, grads[:, h:], extra], axis=1)


def split_class(c):
    return (c // 32, c % 32)


def join_class(x, k):
    hi = x[:, k].astype(jnp.int32)
    lo = x[:, k + 1].astype(jnp.int32)
    return hi * 32 + lo


def coords(L):
    blk, dp = divmod(L, 16)
    yl, x = divmod(blk, 4)
    z, r = divmod(dp, 4)
    yh, c = divmod(r, 2)
    return [x, 2 * yh + yl, z], c


def lin(v, c):
    x, y, z = v
    return ((y % 2) * 4 + x) * 16 + z * 4 + (y // 2) * 2 + c


def train_mate(v):
    return v ^ 1


def test_mate(v):
    return ((((v - 1) % 4) ^ 1) + 1) % 4


def mate_pairs(n, axis, mate):
    out = []
    for L in range(n):
        v, c = coords(L)
        w = list(v)
        w[axis] = mate(v[axis])
        out.append((L, lin(w, c)))
    return out


def core_pairs(n):
    return [(L, L ^ 1) for L in range(n)]


def column_cuts(cols, m):
    tiles = cols // 128
    return [(tiles * p // m) * 128 for p in range(m)] + [cols]


def chain(part, mate, n, order):
    rows = part.shape[0]
    buf = part
    labs = [0]
    for a in order:
        got = lax.ppermute(buf, AXES, mate_pairs(n, a, mate))
        buf = jnp.concatenate([buf, got])
        labs = labs + [o ^ (1 << a) for o in labs]
    at = {o: i for i, o in enumerate(labs)}
    return [buf[at[o] * rows:(at[o] + 1) * rows] for o in range(8)]


def half_gather(shard, mate, n, orders, split=False):
    r, cols = shard.shape
    h = cols // 2
    c = lax.axis_index(AXES) % 2
    mine = lax.dynamic_slice_in_dim(shard, c * h, h, axis=1)
    give = lax.dynamic_slice_in_dim(shard, (1 - c) * h, h, axis=1)
    unit = jnp.concatenate([mine, lax.ppermute(give, AXES, core_pairs(n))])
    cut = column_cuts(h, len(orders))
    parts = [chain(unit[:, cut[p]:cut[p + 1]], mate, n, order) for p, order in enumerate(orders)]
    if split:
        return [jnp.concatenate([b[:r] for b in q] + [b[r:] for b in q]) for q in parts], cut
    blocks = [jnp.concatenate([parts[p][o] for p in range(len(orders))], axis=1) for o in range(8)]
    return jnp.concatenate([b[:r] for b in blocks] + [b[r:] for b in blocks])


def cube_gather(shard, mate, n, orders):
    cut = column_cuts(shard.shape[1], len(orders))
    return jnp.concatenate(
        [chain(shard[:, cut[p]:cut[p + 1]], mate, n, order) for p, order in enumerate(orders)],
        axis=1,
    )


def cube_reduce(blocks, mate, n):
    blocks = list(blocks)
    live = list(range(8))
    for a in range(3):
        send = [o for o in live if o & (1 << a)]
        keep = [o for o in live if not o & (1 << a)]
        rows = blocks[0].shape[0]
        got = lax.ppermute(
            jnp.concatenate([blocks[o] for o in send]), AXES, mate_pairs(n, a, mate)
        )
        for i, o in enumerate(send):
            blocks[o ^ (1 << a)] = blocks[o ^ (1 << a)] + got[i * rows:(i + 1) * rows]
        live = keep
    return blocks[0]


def local(train_grads, train_scale, train_class, test_grads, test_class):
    n = 128
    k = train_grads.shape[1]
    rows = train_grads.shape[0]
    tr = with_side(train_grads, (train_scale,) + split_class(train_class), 0)
    te = with_side(test_grads, split_class(test_class), 4)
    side = k // 2
    te_all = half_gather(te, test_mate, n, THREE)
    tr_cols, cut = half_gather(tr, train_mate, n, TWO, split=True)
    half = 8 * rows

    def partial(lo, hi):
        return sum(
            lax.dot_general(
                t[lo:hi], te_all[:, cut[p]:cut[p + 1]], (((1,), (1,)), ((), ())),
                preferred_element_type=jnp.float32,
            )
            for p, t in enumerate(tr_cols)
        )

    got = lax.ppermute(partial(half, 2 * half), AXES, core_pairs(n))
    own = lax.optimization_barrier(partial(0, half))
    raw = own + jnp.concatenate([got[:, half:], got[:, :half]], axis=1)
    tr_all = tr_cols[-1]
    tr_mine = tr_all[:half]
    tr_side = side - cut[-2]
    scale = tr_mine[:, tr_side].astype(jnp.float32)
    train_hot = indicator(join_class(tr_mine, tr_side + 1))
    test_hot = indicator(join_class(te_all, side + 4))
    w = jnp.tanh(scale[:, None] * raw).astype(jnp.bfloat16)
    part = jnp.dot(w, test_hot, preferred_element_type=jnp.float32)
    per_class = lax.dot_general(
        w, train_hot, (((0,), (0,)), ((), ())), preferred_element_type=jnp.float32
    )
    tp = jnp.sum(per_class * test_hot.astype(jnp.float32), axis=1)
    train_attr = cube_reduce(
        [part[o * rows:(o + 1) * rows] for o in range(8)], train_mate, n
    )
    test_part = tp[:half] + lax.ppermute(tp[half:], AXES, core_pairs(n))
    test_attr = cube_reduce(
        [test_part[o * rows:(o + 1) * rows] for o in range(8)], test_mate, n
    )
    return (train_attr, test_attr)


def solution(mesh):
    in_specs = (
        P(AXES, None),
        P(AXES),
        P(AXES),
        P(AXES, None),
        P(AXES),
    )
    out_specs = (P(AXES, None), P(AXES))
    return jax.shard_map(local, mesh=mesh, in_specs=in_specs, out_specs=out_specs, check_vma=False)
```

```python
import jax
import jax.numpy as jnp
from jax import lax
from jax.sharding import PartitionSpec as P

NCLS = 512
PAD = 128
AXES = ("blk", "dp")
THREE = ((0, 1, 2), (1, 2, 0), (2, 0, 1))
TWO = ((0, 1, 2), (2, 0, 1))


def indicator(labels):
    columns = lax.broadcasted_iota(jnp.int32, (labels.shape[0], NCLS), 1)
    return (labels[:, None] == columns).astype(jnp.bfloat16)


def with_side(grads, side, first):
    rows, k = grads.shape
    cols = lax.broadcasted_iota(jnp.int32, (rows, PAD), 1)
    extra = jnp.zeros((rows, PAD), jnp.bfloat16)
    for j, v in enumerate(side):
        extra = jnp.where(cols == first + j, v[:, None].astype(jnp.bfloat16), extra)
    h = k // 2
    return jnp.concatenate([grads[:, :h], extra, grads[:, h:], extra], axis=1)


def split_class(c):
    return (c // 32, c % 32)


def join_class(x, k):
    hi = x[:, k].astype(jnp.int32)
    lo = x[:, k + 1].astype(jnp.int32)
    return hi * 32 + lo


def coords(L):
    blk, dp = divmod(L, 16)
    yl, x = divmod(blk, 4)
    z, r = divmod(dp, 4)
    yh, c = divmod(r, 2)
    return [x, 2 * yh + yl, z], c


def lin(v, c):
    x, y, z = v
    return ((y % 2) * 4 + x) * 16 + z * 4 + (y // 2) * 2 + c


def train_mate(v):
    return v ^ 1


def test_mate(v):
    return ((((v - 1) % 4) ^ 1) + 1) % 4


def mate_pairs(n, axis, mate):
    out = []
    for L in range(n):
        v, c = coords(L)
        w = list(v)
        w[axis] = mate(v[axis])
        out.append((L, lin(w, c)))
    return out


def core_pairs(n):
    return [(L, L ^ 1) for L in range(n)]


def column_cuts(cols, m):
    tiles = cols // 128
    return [(tiles * p // m) * 128 for p in range(m)] + [cols]


def chain(part, mate, n, order, first=None):
    rows = part.shape[0]
    buf = part
    labs = [0]
    if first is not None:
        buf = jnp.concatenate([buf, first])
        labs = [0, 1 << order[0]]
        order = order[1:]
    for a in order:
        got = lax.ppermute(buf, AXES, mate_pairs(n, a, mate))
        buf = jnp.concatenate([buf, got])
        labs = labs + [o ^ (1 << a) for o in labs]
    at = {o: i for i, o in enumerate(labs)}
    return [buf[at[o] * rows:(at[o] + 1) * rows] for o in range(8)]


def half_unit(shard, n):
    h = shard.shape[1] // 2
    c = lax.axis_index(AXES) % 2
    mine = lax.dynamic_slice_in_dim(shard, c * h, h, axis=1)
    give = lax.dynamic_slice_in_dim(shard, (1 - c) * h, h, axis=1)
    return jnp.concatenate([mine, lax.ppermute(give, AXES, core_pairs(n))])


def half_gather(pieces, mate, n, orders, firsts=None):
    r = pieces[0].shape[0] // 2
    firsts = firsts or [None] * len(orders)
    parts = [chain(q, mate, n, order, f) for q, order, f in zip(pieces, orders, firsts)]
    blocks = [jnp.concatenate([parts[p][o] for p in range(len(orders))], axis=1) for o in range(8)]
    return jnp.concatenate([b[:r] for b in blocks] + [b[r:] for b in blocks])


def column_pieces(unit, m):
    cut = column_cuts(unit.shape[1], m)
    return [unit[:, cut[p]:cut[p + 1]] for p in range(m)]


def cube_reduce(blocks, mate, n):
    blocks = list(blocks)
    live = list(range(8))
    for a in range(3):
        send = [o for o in live if o & (1 << a)]
        keep = [o for o in live if not o & (1 << a)]
        rows = blocks[0].shape[0]
        got = lax.ppermute(
            jnp.concatenate([blocks[o] for o in send]), AXES, mate_pairs(n, a, mate)
        )
        for i, o in enumerate(send):
            blocks[o ^ (1 << a)] = blocks[o ^ (1 << a)] + got[i * rows:(i + 1) * rows]
        live = keep
    return blocks[0]


def local(train_grads, train_scale, train_class, test_grads, test_class):
    n = 128
    k = train_grads.shape[1]
    rows = train_grads.shape[0]
    tr = with_side(train_grads, (train_scale,) + split_class(train_class), 0)
    te = with_side(test_grads, split_class(test_class), 4)
    side = k // 2
    tr_pieces = column_pieces(half_unit(tr, n), len(TWO))
    tr_first = [
        lax.ppermute(q, AXES, mate_pairs(n, order[0], train_mate))
        for q, order in zip(tr_pieces, TWO)
    ]
    te_unit, tr_first = lax.optimization_barrier((half_unit(te, n), tr_first))
    tr_all = half_gather(tr_pieces, train_mate, n, TWO, tr_first)
    te_all = half_gather(column_pieces(te_unit, len(THREE)), test_mate, n, THREE)
    half = 8 * rows

    def partial(t):
        return lax.dot_general(
            t, te_all, (((1,), (1,)), ((), ())), preferred_element_type=jnp.float32
        )

    got = lax.ppermute(partial(tr_all[half:]), AXES, core_pairs(n))
    own = lax.optimization_barrier(partial(tr_all[:half]))
    raw = own + jnp.concatenate([got[:, half:], got[:, :half]], axis=1)
    tr_mine = tr_all[:half]
    scale = tr_mine[:, side].astype(jnp.float32)
    train_hot = indicator(join_class(tr_mine, side + 1))
    test_hot = indicator(join_class(te_all, side + 4))
    w = jnp.tanh(scale[:, None] * raw).astype(jnp.bfloat16)
    part = jnp.dot(w, test_hot, preferred_element_type=jnp.float32)
    per_class = lax.dot_general(
        w, train_hot, (((0,), (0,)), ((), ())), preferred_element_type=jnp.float32
    )
    tp = jnp.sum(per_class * test_hot.astype(jnp.float32), axis=1)
    train_attr = cube_reduce(
        [part[o * rows:(o + 1) * rows] for o in range(8)], train_mate, n
    )
    test_part = tp[:half] + lax.ppermute(tp[half:], AXES, core_pairs(n))
    test_attr = cube_reduce(
        [test_part[o * rows:(o + 1) * rows] for o in range(8)], test_mate, n
    )
    return (train_attr, test_attr)


def solution(mesh):
    in_specs = (
        P(AXES, None),
        P(AXES),
        P(AXES),
        P(AXES, None),
        P(AXES),
    )
    out_specs = (P(AXES, None), P(AXES))
    return jax.shard_map(local, mesh=mesh, in_specs=in_specs, out_specs=out_specs, check_vma=False)
```

```python
import jax
import jax.numpy as jnp
from jax import lax
from jax.sharding import PartitionSpec as P

NCLS = 512
PAD = 128
AXES = ("blk", "dp")
THREE = ((0, 1, 2), (1, 2, 0), (2, 0, 1))
TWO = ((0, 1, 2), (2, 0, 1))


def indicator(labels):
    columns = lax.broadcasted_iota(jnp.int32, (labels.shape[0], NCLS), 1)
    return (labels[:, None] == columns).astype(jnp.bfloat16)


def with_side(grads, side, first):
    rows, k = grads.shape
    cols = lax.broadcasted_iota(jnp.int32, (rows, PAD), 1)
    extra = jnp.zeros((rows, PAD), jnp.bfloat16)
    for j, v in enumerate(side):
        extra = jnp.where(cols == first + j, v[:, None].astype(jnp.bfloat16), extra)
    h = k // 2
    return jnp.concatenate([grads[:, :h], extra, grads[:, h:], extra], axis=1)


def split_class(c):
    return (c // 32, c % 32)


def join_class(x, k):
    hi = x[:, k].astype(jnp.int32)
    lo = x[:, k + 1].astype(jnp.int32)
    return hi * 32 + lo


def coords(L):
    blk, dp = divmod(L, 16)
    yl, x = divmod(blk, 4)
    z, r = divmod(dp, 4)
    yh, c = divmod(r, 2)
    return [x, 2 * yh + yl, z], c


def lin(v, c):
    x, y, z = v
    return ((y % 2) * 4 + x) * 16 + z * 4 + (y // 2) * 2 + c


def train_mate(v):
    return v ^ 1


def test_mate(v):
    return ((((v - 1) % 4) ^ 1) + 1) % 4


def mate_pairs(n, axis, mate):
    out = []
    for L in range(n):
        v, c = coords(L)
        w = list(v)
        w[axis] = mate(v[axis])
        out.append((L, lin(w, c)))
    return out


def core_pairs(n):
    return [(L, L ^ 1) for L in range(n)]


def column_cuts(cols, m):
    tiles = cols // 128
    return [(tiles * p // m) * 128 for p in range(m)] + [cols]


def chain(part, mate, n, order):
    rows = part.shape[0]
    buf = part
    labs = [0]
    for a in order:
        got = lax.ppermute(buf, AXES, mate_pairs(n, a, mate))
        buf = jnp.concatenate([buf, got])
        labs = labs + [o ^ (1 << a) for o in labs]
    at = {o: i for i, o in enumerate(labs)}
    return [buf[at[o] * rows:(at[o] + 1) * rows] for o in range(8)]


def half_gather(shard, mate, n, orders):
    r, cols = shard.shape
    h = cols // 2
    c = lax.axis_index(AXES) % 2
    mine = lax.dynamic_slice_in_dim(shard, c * h, h, axis=1)
    give = lax.dynamic_slice_in_dim(shard, (1 - c) * h, h, axis=1)
    unit = jnp.concatenate([mine, lax.ppermute(give, AXES, core_pairs(n))])
    cut = column_cuts(h, len(orders))
    parts = [chain(unit[:, cut[p]:cut[p + 1]], mate, n, order) for p, order in enumerate(orders)]
    blocks = [jnp.concatenate([parts[p][o] for p in range(len(orders))], axis=1) for o in range(8)]
    return jnp.concatenate([b[:r] for b in blocks] + [b[r:] for b in blocks])


def cube_gather(shard, mate, n, orders):
    cut = column_cuts(shard.shape[1], len(orders))
    return jnp.concatenate(
        [chain(shard[:, cut[p]:cut[p + 1]], mate, n, order) for p, order in enumerate(orders)],
        axis=1,
    )


def cube_reduce(blocks, mate, n):
    blocks = list(blocks)
    live = list(range(8))
    for a in range(3):
        send = [o for o in live if o & (1 << a)]
        keep = [o for o in live if not o & (1 << a)]
        rows = blocks[0].shape[0]
        got = lax.ppermute(
            jnp.concatenate([blocks[o] for o in send]), AXES, mate_pairs(n, a, mate)
        )
        for i, o in enumerate(send):
            blocks[o ^ (1 << a)] = blocks[o ^ (1 << a)] + got[i * rows:(i + 1) * rows]
        live = keep
    return blocks[0]


def offset_pairs(n, o, mate):
    out = []
    for L in range(n):
        v, c = coords(L)
        w = [mate(v[a]) if o & (1 << a) else v[a] for a in range(3)]
        out.append((L, lin(w, c)))
    return out


def cube_reduce_square(blocks, mate, n):
    blocks = list(blocks)
    rows = blocks[0].shape[0]
    for m in (1, 2, 3):
        send = [o for o in range(8) if o & 3 == m]
        got = lax.ppermute(jnp.concatenate([blocks[o] for o in send]), AXES, offset_pairs(n, m, mate))
        for i, o in enumerate(send):
            blocks[o ^ m] = blocks[o ^ m] + got[i * rows:(i + 1) * rows]
    got = lax.ppermute(blocks[4], AXES, offset_pairs(n, 4, mate))
    return blocks[0] + got


def local(train_grads, train_scale, train_class, test_grads, test_class):
    n = 128
    k = train_grads.shape[1]
    rows = train_grads.shape[0]
    tr = with_side(train_grads, (train_scale,) + split_class(train_class), 0)
    te = with_side(test_grads, split_class(test_class), 4)
    side = k // 2
    te_all = half_gather(te, test_mate, n, THREE)
    tr_all = half_gather(tr, train_mate, n, TWO)
    half = 8 * rows

    def partial(t):
        return lax.dot_general(
            t, te_all, (((1,), (1,)), ((), ())), preferred_element_type=jnp.float32
        )

    got = lax.ppermute(partial(tr_all[half:]), AXES, core_pairs(n))
    own = lax.optimization_barrier(partial(tr_all[:half]))
    raw = own + jnp.concatenate([got[:, half:], got[:, :half]], axis=1)
    tr_mine = tr_all[:half]
    scale = tr_mine[:, side].astype(jnp.float32)
    train_hot = indicator(join_class(tr_mine, side + 1))
    test_hot = indicator(join_class(te_all, side + 4))
    w = jnp.tanh(scale[:, None] * raw).astype(jnp.bfloat16)
    part = jnp.dot(w, test_hot, preferred_element_type=jnp.float32)
    per_class = lax.dot_general(
        w, train_hot, (((0,), (0,)), ((), ())), preferred_element_type=jnp.float32
    )
    tp = jnp.sum(per_class * test_hot.astype(jnp.float32), axis=1)
    train_attr = cube_reduce_square(
        [part[o * rows:(o + 1) * rows] for o in range(8)], train_mate, n
    )
    test_part = tp[:half] + lax.ppermute(tp[half:], AXES, core_pairs(n))
    test_attr = cube_reduce(
        [test_part[o * rows:(o + 1) * rows] for o in range(8)], test_mate, n
    )
    return (train_attr, test_attr)


def solution(mesh):
    in_specs = (
        P(AXES, None),
        P(AXES),
        P(AXES),
        P(AXES, None),
        P(AXES),
    )
    out_specs = (P(AXES, None), P(AXES))
    return jax.shard_map(local, mesh=mesh, in_specs=in_specs, out_specs=out_specs, check_vma=False)
```

```python
import jax
import jax.numpy as jnp
from jax import lax
from jax.sharding import PartitionSpec as P

NCLS = 512
PAD = 128
AXES = ("blk", "dp")
THREE = ((0, 1, 2), (1, 2, 0), (2, 0, 1))
TWO = ((0, 1, 2), (2, 0, 1))


def indicator(labels):
    columns = lax.broadcasted_iota(jnp.int32, (labels.shape[0], NCLS), 1)
    return (labels[:, None] == columns).astype(jnp.bfloat16)


def with_side(grads, side, first):
    rows, k = grads.shape
    cols = lax.broadcasted_iota(jnp.int32, (rows, PAD), 1)
    extra = jnp.zeros((rows, PAD), jnp.bfloat16)
    for j, v in enumerate(side):
        extra = jnp.where(cols == first + j, v[:, None].astype(jnp.bfloat16), extra)
    h = k // 2
    return jnp.concatenate([grads[:, :h], extra, grads[:, h:], extra], axis=1)


def split_class(c):
    return (c // 32, c % 32)


def join_class(x, k):
    hi = x[:, k].astype(jnp.int32)
    lo = x[:, k + 1].astype(jnp.int32)
    return hi * 32 + lo


def coords(L):
    blk, dp = divmod(L, 16)
    yl, x = divmod(blk, 4)
    z, r = divmod(dp, 4)
    yh, c = divmod(r, 2)
    return [x, 2 * yh + yl, z], c


def lin(v, c):
    x, y, z = v
    return ((y % 2) * 4 + x) * 16 + z * 4 + (y // 2) * 2 + c


def train_mate(v):
    return v ^ 1


def test_mate(v):
    return ((((v - 1) % 4) ^ 1) + 1) % 4


def mate_pairs(n, axis, mate):
    out = []
    for L in range(n):
        v, c = coords(L)
        w = list(v)
        w[axis] = mate(v[axis])
        out.append((L, lin(w, c)))
    return out


def core_pairs(n):
    return [(L, L ^ 1) for L in range(n)]


def column_cuts(cols, m):
    tiles = cols // 128
    return [(tiles * p // m) * 128 for p in range(m)] + [cols]


def chain(part, mate, n, order):
    rows = part.shape[0]
    buf = part
    labs = [0]
    for a in order:
        got = lax.ppermute(buf, AXES, mate_pairs(n, a, mate))
        buf = jnp.concatenate([buf, got])
        labs = labs + [o ^ (1 << a) for o in labs]
    at = {o: i for i, o in enumerate(labs)}
    return [buf[at[o] * rows:(at[o] + 1) * rows] for o in range(8)]


def half_gather(shard, mate, n, orders):
    r, cols = shard.shape
    h = cols // 2
    c = lax.axis_index(AXES) % 2
    mine = lax.dynamic_slice_in_dim(shard, c * h, h, axis=1)
    give = lax.dynamic_slice_in_dim(shard, (1 - c) * h, h, axis=1)
    unit = jnp.concatenate([mine, lax.ppermute(give, AXES, core_pairs(n))])
    cut = column_cuts(h, len(orders))
    parts = [chain(unit[:, cut[p]:cut[p + 1]], mate, n, order) for p, order in enumerate(orders)]
    blocks = [jnp.concatenate([parts[p][o] for p in range(len(orders))], axis=1) for o in range(8)]
    return jnp.concatenate([b[:r] for b in blocks] + [b[r:] for b in blocks])


def cube_gather(shard, mate, n, orders):
    cut = column_cuts(shard.shape[1], len(orders))
    return jnp.concatenate(
        [chain(shard[:, cut[p]:cut[p + 1]], mate, n, order) for p, order in enumerate(orders)],
        axis=1,
    )


def cube_reduce(blocks, mate, n):
    blocks = list(blocks)
    live = list(range(8))
    for a in range(3):
        send = [o for o in live if o & (1 << a)]
        keep = [o for o in live if not o & (1 << a)]
        rows = blocks[0].shape[0]
        got = lax.ppermute(
            jnp.concatenate([blocks[o] for o in send]), AXES, mate_pairs(n, a, mate)
        )
        for i, o in enumerate(send):
            blocks[o ^ (1 << a)] = blocks[o ^ (1 << a)] + got[i * rows:(i + 1) * rows]
        live = keep
    return blocks[0]


def offset_pairs(n, o, mate):
    out = []
    for L in range(n):
        v, c = coords(L)
        w = [mate(v[a]) if o & (1 << a) else v[a] for a in range(3)]
        out.append((L, lin(w, c)))
    return out


def cube_reduce_square(blocks, mate, n):
    blocks = list(blocks)
    rows = blocks[0].shape[0]
    for m in (1, 2, 3):
        send = [o for o in range(8) if o & 3 == m]
        got = lax.ppermute(jnp.concatenate([blocks[o] for o in send]), AXES, offset_pairs(n, m, mate))
        for i, o in enumerate(send):
            blocks[o ^ m] = blocks[o ^ m] + got[i * rows:(i + 1) * rows]
    got = lax.ppermute(blocks[4], AXES, offset_pairs(n, 4, mate))
    return blocks[0] + got


def local(train_grads, train_scale, train_class, test_grads, test_class):
    n = 128
    k = train_grads.shape[1]
    rows = train_grads.shape[0]
    tr = with_side(train_grads, (train_scale,) + split_class(train_class), 0)
    te = with_side(test_grads, split_class(test_class), 4)
    side = k // 2
    te_all = half_gather(te, test_mate, n, THREE)
    tr_all = half_gather(tr, train_mate, n, TWO)
    half = 8 * rows

    def partial(t):
        return lax.dot_general(
            t, te_all, (((1,), (1,)), ((), ())), preferred_element_type=jnp.float32
        )

    got = lax.ppermute(partial(tr_all[half:]), AXES, core_pairs(n))
    own = lax.optimization_barrier(partial(tr_all[:half]))
    raw = own + jnp.concatenate([got[:, half:], got[:, :half]], axis=1)
    tr_mine = tr_all[:half]
    scale = tr_mine[:, side].astype(jnp.float32)
    train_hot = indicator(join_class(tr_mine, side + 1))
    test_hot = indicator(join_class(te_all, side + 4))
    w = jnp.tanh(scale[:, None] * raw).astype(jnp.bfloat16)
    part = jnp.dot(w, test_hot, preferred_element_type=jnp.float32)
    per_class = lax.dot_general(
        w, train_hot, (((0,), (0,)), ((), ())), preferred_element_type=jnp.float32
    )
    tp = jnp.sum(per_class * test_hot.astype(jnp.float32), axis=1)
    train_attr = cube_reduce_square(
        [part[o * rows:(o + 1) * rows] for o in range(8)], train_mate, n
    )
    test_part = tp[:half] + lax.ppermute(tp[half:], AXES, core_pairs(n))
    test_attr = cube_reduce_square(
        [test_part[o * rows:(o + 1) * rows] for o in range(8)], test_mate, n
    )
    return (train_attr, test_attr)


def solution(mesh):
    in_specs = (
        P(AXES, None),
        P(AXES),
        P(AXES),
        P(AXES, None),
        P(AXES),
    )
    out_specs = (P(AXES, None), P(AXES))
    return jax.shard_map(local, mesh=mesh, in_specs=in_specs, out_specs=out_specs, check_vma=False)
```

```python
import jax
import jax.numpy as jnp
from jax import lax
from jax.sharding import PartitionSpec as P

NCLS = 512
PAD = 128
AXES = ("blk", "dp")
THREE = ((0, 1, 2), (1, 2, 0), (2, 0, 1))
TWO = ((0, 1, 2), (2, 0, 1))


def indicator(labels):
    columns = lax.broadcasted_iota(jnp.int32, (labels.shape[0], NCLS), 1)
    return (labels[:, None] == columns).astype(jnp.bfloat16)


def with_side(grads, side, first):
    rows, k = grads.shape
    cols = lax.broadcasted_iota(jnp.int32, (rows, PAD), 1)
    extra = jnp.zeros((rows, PAD), jnp.bfloat16)
    for j, v in enumerate(side):
        extra = jnp.where(cols == first + j, v[:, None].astype(jnp.bfloat16), extra)
    h = k // 2
    return jnp.concatenate([grads[:, :h], extra, grads[:, h:], extra], axis=1)


def split_class(c):
    return (c // 32, c % 32)


def join_class(x, k):
    hi = x[:, k].astype(jnp.int32)
    lo = x[:, k + 1].astype(jnp.int32)
    return hi * 32 + lo


def coords(L):
    blk, dp = divmod(L, 16)
    yl, x = divmod(blk, 4)
    z, r = divmod(dp, 4)
    yh, c = divmod(r, 2)
    return [x, 2 * yh + yl, z], c


def lin(v, c):
    x, y, z = v
    return ((y % 2) * 4 + x) * 16 + z * 4 + (y // 2) * 2 + c


def train_mate(v):
    return v ^ 1


def test_mate(v):
    return ((((v - 1) % 4) ^ 1) + 1) % 4


def mate_pairs(n, axis, mate):
    out = []
    for L in range(n):
        v, c = coords(L)
        w = list(v)
        w[axis] = mate(v[axis])
        out.append((L, lin(w, c)))
    return out


def core_pairs(n):
    return [(L, L ^ 1) for L in range(n)]


def column_cuts(cols, m):
    tiles = cols // 128
    return [(tiles * p // m) * 128 for p in range(m)] + [cols]


def chain(part, mate, n, order):
    rows = part.shape[0]
    buf = part
    labs = [0]
    for a in order:
        got = lax.ppermute(buf, AXES, mate_pairs(n, a, mate))
        buf = jnp.concatenate([buf, got])
        labs = labs + [o ^ (1 << a) for o in labs]
    at = {o: i for i, o in enumerate(labs)}
    return [buf[at[o] * rows:(at[o] + 1) * rows] for o in range(8)]


def half_gather(shard, mate, n, orders):
    r, cols = shard.shape
    h = cols // 2
    c = lax.axis_index(AXES) % 2
    mine = lax.dynamic_slice_in_dim(shard, c * h, h, axis=1)
    give = lax.dynamic_slice_in_dim(shard, (1 - c) * h, h, axis=1)
    unit = jnp.concatenate([mine, lax.ppermute(give, AXES, core_pairs(n))])
    cut = column_cuts(h, len(orders))
    parts = [chain(unit[:, cut[p]:cut[p + 1]], mate, n, order) for p, order in enumerate(orders)]
    blocks = [jnp.concatenate([parts[p][o] for p in range(len(orders))], axis=1) for o in range(8)]
    return jnp.concatenate([b[:r] for b in blocks] + [b[r:] for b in blocks])


def cube_gather(shard, mate, n, orders):
    cut = column_cuts(shard.shape[1], len(orders))
    return jnp.concatenate(
        [chain(shard[:, cut[p]:cut[p + 1]], mate, n, order) for p, order in enumerate(orders)],
        axis=1,
    )


def cube_reduce(blocks, mate, n):
    blocks = list(blocks)
    live = list(range(8))
    for a in range(3):
        send = [o for o in live if o & (1 << a)]
        keep = [o for o in live if not o & (1 << a)]
        rows = blocks[0].shape[0]
        got = lax.ppermute(
            jnp.concatenate([blocks[o] for o in send]), AXES, mate_pairs(n, a, mate)
        )
        for i, o in enumerate(send):
            blocks[o ^ (1 << a)] = blocks[o ^ (1 << a)] + got[i * rows:(i + 1) * rows]
        live = keep
    return blocks[0]


def offset_pairs(n, o, mate):
    out = []
    for L in range(n):
        v, c = coords(L)
        w = [mate(v[a]) if o & (1 << a) else v[a] for a in range(3)]
        out.append((L, lin(w, c)))
    return out


def cube_reduce_square(blocks, mate, n):
    blocks = list(blocks)
    rows = blocks[0].shape[0]
    for m in (1, 2, 3):
        send = [o for o in range(8) if o & 3 == m]
        got = lax.ppermute(jnp.concatenate([blocks[o] for o in send]), AXES, offset_pairs(n, m, mate))
        for i, o in enumerate(send):
            blocks[o ^ m] = blocks[o ^ m] + got[i * rows:(i + 1) * rows]
    got = lax.ppermute(blocks[4], AXES, offset_pairs(n, 4, mate))
    return blocks[0] + got


def local(train_grads, train_scale, train_class, test_grads, test_class):
    n = 128
    k = train_grads.shape[1]
    rows = train_grads.shape[0]
    tr = with_side(train_grads, (train_scale,) + split_class(train_class), 0)
    te = with_side(test_grads, split_class(test_class), 4)
    side = k // 2
    te_all = half_gather(te, test_mate, n, THREE)
    tr_all = half_gather(tr, train_mate, n, TWO)
    half = 8 * rows

    def partial(t):
        return lax.dot_general(
            t, te_all, (((1,), (1,)), ((), ())), preferred_element_type=jnp.float32
        )

    tr_mine = tr_all[:half]
    scale = tr_mine[:, side].astype(jnp.float32)
    train_hot = indicator(join_class(tr_mine, side + 1))
    test_hot = indicator(join_class(te_all, side + 4))
    q = half // 2

    def weights(lo, hi):
        got = lax.ppermute(partial(tr_all[half + lo:half + hi]), AXES, core_pairs(n))
        own = lax.optimization_barrier(partial(tr_all[lo:hi]))
        raw = own + jnp.concatenate([got[:, half:], got[:, :half]], axis=1)
        return jnp.tanh(scale[lo:hi, None] * raw).astype(jnp.bfloat16)

    w_hi = weights(q, half)
    part_hi = jnp.dot(w_hi, test_hot, preferred_element_type=jnp.float32)
    from_z = lax.ppermute(part_hi, AXES, offset_pairs(n, 4, train_mate))
    w_lo = weights(0, q)
    part_lo = jnp.dot(w_lo, test_hot, preferred_element_type=jnp.float32) + from_z
    blocks = [part_lo[o * rows:(o + 1) * rows] for o in range(4)]
    for m in (1, 2, 3):
        blocks[0] = blocks[0] + lax.ppermute(blocks[m], AXES, offset_pairs(n, m, train_mate))
    train_attr = blocks[0]
    per_class = lax.dot_general(
        w_lo, train_hot[:q], (((0,), (0,)), ((), ())), preferred_element_type=jnp.float32
    ) + lax.dot_general(
        w_hi, train_hot[q:], (((0,), (0,)), ((), ())), preferred_element_type=jnp.float32
    )
    tp = jnp.sum(per_class * test_hot.astype(jnp.float32), axis=1)
    test_part = tp[:half] + lax.ppermute(tp[half:], AXES, core_pairs(n))
    test_attr = cube_reduce(
        [test_part[o * rows:(o + 1) * rows] for o in range(8)], test_mate, n
    )
    return (train_attr, test_attr)


def solution(mesh):
    in_specs = (
        P(AXES, None),
        P(AXES),
        P(AXES),
        P(AXES, None),
        P(AXES),
    )
    out_specs = (P(AXES, None), P(AXES))
    return jax.shard_map(local, mesh=mesh, in_specs=in_specs, out_specs=out_specs, check_vma=False)
```

```python
import jax
import jax.numpy as jnp
from jax import lax
from jax.sharding import PartitionSpec as P

NCLS = 512
PAD = 128
AXES = ("blk", "dp")
THREE = ((0, 1, 2), (1, 2, 0), (2, 0, 1))
TWO = ((0, 1, 2), (2, 0, 1))


def indicator(labels):
    columns = lax.broadcasted_iota(jnp.int32, (labels.shape[0], NCLS), 1)
    return (labels[:, None] == columns).astype(jnp.bfloat16)


def with_side(grads, side, first):
    rows, k = grads.shape
    cols = lax.broadcasted_iota(jnp.int32, (rows, PAD), 1)
    extra = jnp.zeros((rows, PAD), jnp.bfloat16)
    for j, v in enumerate(side):
        extra = jnp.where(cols == first + j, v[:, None].astype(jnp.bfloat16), extra)
    return grads, extra


def split_class(c):
    return (c // 32, c % 32)


def join_class(x, k):
    hi = x[:, k].astype(jnp.int32)
    lo = x[:, k + 1].astype(jnp.int32)
    return hi * 32 + lo


def coords(L):
    blk, dp = divmod(L, 16)
    yl, x = divmod(blk, 4)
    z, r = divmod(dp, 4)
    yh, c = divmod(r, 2)
    return [x, 2 * yh + yl, z], c


def lin(v, c):
    x, y, z = v
    return ((y % 2) * 4 + x) * 16 + z * 4 + (y // 2) * 2 + c


def train_mate(v):
    return v ^ 1


def test_mate(v):
    return ((((v - 1) % 4) ^ 1) + 1) % 4


def mate_pairs(n, axis, mate):
    out = []
    for L in range(n):
        v, c = coords(L)
        w = list(v)
        w[axis] = mate(v[axis])
        out.append((L, lin(w, c)))
    return out


def core_pairs(n):
    return [(L, L ^ 1) for L in range(n)]


def column_cuts(cols, m):
    tiles = cols // 128
    return [(tiles * p // m) * 128 for p in range(m)] + [cols]


def chain(part, mate, n, order):
    rows = part.shape[0]
    buf = part
    labs = [0]
    for a in order:
        got = lax.ppermute(buf, AXES, mate_pairs(n, a, mate))
        buf = jnp.concatenate([buf, got])
        labs = labs + [o ^ (1 << a) for o in labs]
    at = {o: i for i, o in enumerate(labs)}
    return [buf[at[o] * rows:(at[o] + 1) * rows] for o in range(8)]


def half_gather(shard, mate, n, orders):
    grads, extra = shard
    r, k = grads.shape
    h = k // 2 + extra.shape[1]
    c = lax.axis_index(AXES) % 2
    mine = jnp.concatenate([lax.dynamic_slice_in_dim(grads, c * (k // 2), k // 2, axis=1), extra], axis=1)
    give = jnp.concatenate([lax.dynamic_slice_in_dim(grads, (1 - c) * (k // 2), k // 2, axis=1), extra], axis=1)
    unit = jnp.concatenate([mine, lax.ppermute(give, AXES, core_pairs(n))])
    cut = column_cuts(h, len(orders))
    parts = [chain(unit[:, cut[p]:cut[p + 1]], mate, n, order) for p, order in enumerate(orders)]
    blocks = [jnp.concatenate([parts[p][o] for p in range(len(orders))], axis=1) for o in range(8)]
    return jnp.concatenate([b[:r] for b in blocks] + [b[r:] for b in blocks])


def cube_gather(shard, mate, n, orders):
    cut = column_cuts(shard.shape[1], len(orders))
    return jnp.concatenate(
        [chain(shard[:, cut[p]:cut[p + 1]], mate, n, order) for p, order in enumerate(orders)],
        axis=1,
    )


def cube_reduce(blocks, mate, n):
    blocks = list(blocks)
    live = list(range(8))
    for a in range(3):
        send = [o for o in live if o & (1 << a)]
        keep = [o for o in live if not o & (1 << a)]
        rows = blocks[0].shape[0]
        got = lax.ppermute(
            jnp.concatenate([blocks[o] for o in send]), AXES, mate_pairs(n, a, mate)
        )
        for i, o in enumerate(send):
            blocks[o ^ (1 << a)] = blocks[o ^ (1 << a)] + got[i * rows:(i + 1) * rows]
        live = keep
    return blocks[0]


def offset_pairs(n, o, mate):
    out = []
    for L in range(n):
        v, c = coords(L)
        w = [mate(v[a]) if o & (1 << a) else v[a] for a in range(3)]
        out.append((L, lin(w, c)))
    return out


def cube_reduce_square(blocks, mate, n):
    blocks = list(blocks)
    rows = blocks[0].shape[0]
    for m in (1, 2, 3):
        send = [o for o in range(8) if o & 3 == m]
        got = lax.ppermute(jnp.concatenate([blocks[o] for o in send]), AXES, offset_pairs(n, m, mate))
        for i, o in enumerate(send):
            blocks[o ^ m] = blocks[o ^ m] + got[i * rows:(i + 1) * rows]
    got = lax.ppermute(blocks[4], AXES, offset_pairs(n, 4, mate))
    return blocks[0] + got


def local(train_grads, train_scale, train_class, test_grads, test_class):
    n = 128
    k = train_grads.shape[1]
    rows = train_grads.shape[0]
    tr = with_side(train_grads, (train_scale,) + split_class(train_class), 0)
    te = with_side(test_grads, split_class(test_class), 4)
    side = k // 2
    te_all = half_gather(te, test_mate, n, THREE)
    tr_all = half_gather(tr, train_mate, n, TWO)
    half = 8 * rows

    def partial(t):
        return lax.dot_general(
            t, te_all, (((1,), (1,)), ((), ())), preferred_element_type=jnp.float32
        )

    got = lax.ppermute(partial(tr_all[half:]), AXES, core_pairs(n))
    own = lax.optimization_barrier(partial(tr_all[:half]))
    raw = own + jnp.concatenate([got[:, half:], got[:, :half]], axis=1)
    tr_mine = tr_all[:half]
    scale = tr_mine[:, side].astype(jnp.float32)
    train_hot = indicator(join_class(tr_mine, side + 1))
    test_hot = indicator(join_class(te_all, side + 4))
    w = jnp.tanh(scale[:, None] * raw).astype(jnp.bfloat16)
    part = jnp.dot(w, test_hot, preferred_element_type=jnp.float32)
    per_class = lax.dot_general(
        w, train_hot, (((0,), (0,)), ((), ())), preferred_element_type=jnp.float32
    )
    tp = jnp.sum(per_class * test_hot.astype(jnp.float32), axis=1)
    train_attr = cube_reduce_square(
        [part[o * rows:(o + 1) * rows] for o in range(8)], train_mate, n
    )
    test_part = tp[:half] + lax.ppermute(tp[half:], AXES, core_pairs(n))
    test_attr = cube_reduce(
        [test_part[o * rows:(o + 1) * rows] for o in range(8)], test_mate, n
    )
    return (train_attr, test_attr)


def solution(mesh):
    in_specs = (
        P(AXES, None),
        P(AXES),
        P(AXES),
        P(AXES, None),
        P(AXES),
    )
    out_specs = (P(AXES, None), P(AXES))
    return jax.shard_map(local, mesh=mesh, in_specs=in_specs, out_specs=out_specs, check_vma=False)
```
